32 devices in a mesh: rows: 8 (over z, x), cols: 4 (over y, core).
Axes of the slice: x: 2, y: 2, z: 4, core: 2. Of those that a mesh axis runs over, the one named last changes fastest.
Arguments:
- matrix: float32 [1, 256, 6144], P(None, 'cols', 'rows'), may hold values from -110 to 110, as said below
Outputs:
- updated: float32 [1, 256, 6144], P(None, 'cols', 'rows')
The draws below stay inside these ranges and needn't reach their ends.
Inputs may be any that keep to these rules, and one draw needn't show every extreme that they name: Every 64-column panel has full column rank, and for each panel k the matrix I - top_k has all singular values at least 0.5.
All inputs are finite; a program needn't handle non-finite values.
Results may differ from the reference program's by a relative error of at most 0.00019.
Values sent between devices are 32-bit elements; how exact they have to be, the bound alone decides.
No kernel may reach another device: no remote copies, remote signals or barrier semaphores. Data moves between devices by JAX's collectives and lax.ppermute only.
A program may use at most 64 MiB of HBM per device.

```python
import math
import jax
import jax.numpy as jnp
from jax import lax

B = 64
BLK_DEV = 1
ROWS = 6144
GROUP = 256


def draw_matrix(key, part):
    key_base = jax.random.fold_in(key, 101)
    key_rough = jax.random.fold_in(key, 202)
    key_column = jax.random.fold_in(key, 303)
    shape = (BLK_DEV, GROUP, ROWS)
    position = jnp.arange(ROWS, dtype=jnp.float32) / ROWS
    rough = jnp.exp(jax.random.uniform(key_rough, (ROWS,), jnp.float32, 0.0, math.log(10.0)))
    column_scale = jnp.exp(jax.random.uniform(key_column, (BLK_DEV, GROUP, 1), jnp.float32, math.log(0.3), math.log(3.0)))
    values = jax.random.truncated_normal(key_base, -6.0, 6.0, shape, jnp.float32) * (1.0 + 2.0 * position)
    return 0.1 * values * rough * column_scale


def setup_inputs(seed: int = 0) -> dict:
    arg_keys = jax.random.split(jax.random.key(seed), 2)
    return {
        "matrix": draw_matrix(jax.random.fold_in(arg_keys[1], 71), 0),
    }


def reference(matrix):
    block_count, group_width, total_rows = matrix.shape
    current = matrix.reshape(block_count * group_width, total_rows)
    positions = jnp.arange(total_rows, dtype=jnp.int32)
    identity = jnp.eye(B, dtype=jnp.float32)
    highest = lax.Precision.HIGHEST
    for panel_index in range(2):
        offset = panel_index * B
        panel = current[offset:offset + B]
        panel = jnp.where((positions >= offset)[None, :], panel, jnp.zeros_like(panel))
        gram = jnp.dot(panel, panel.T, precision=highest)
        factor = jnp.linalg.cholesky(gram)
        basis = lax.linalg.triangular_solve(factor, panel, left_side=True, lower=True)
        top_block = basis[:, offset:offset + B]
        inverse = jnp.linalg.inv(identity - top_block.T)
        unit_rows = jnp.zeros((B, total_rows), jnp.float32).at[:, offset:offset + B].set(identity)
        reflect = unit_rows - basis
        products = jnp.dot(reflect, current.T, precision=highest)
        mixed = jnp.dot(inverse, products, precision=highest)
        current = current - jnp.dot(mixed.T, reflect, precision=highest)
    return current.reshape(block_count, group_width, total_rows)
```

```python
import jax
import jax.numpy as jnp
from jax import lax
from jax.sharding import PartitionSpec as P

HIGHEST_PRECISION = lax.Precision.HIGHEST


def inner_rows(left, right):
    return lax.dot_general(left, right, (((1,), (1,)), ((), ())), precision=HIGHEST_PRECISION)


def apply_left(square, right_side):
    return jnp.dot(square, right_side, precision=HIGHEST_PRECISION)


def butterfly_sum(x, axis, size):
    if size & (size - 1):
        return lax.psum(x, axis)
    step = 1
    while step < size:
        x = x + lax.ppermute(x, axis, [(i, i ^ step) for i in range(size)])
        step *= 2
    return x


def invert_near_identity(square):
    identity = jnp.eye(square.shape[0], dtype=jnp.float32)
    approx = square.T * (2.0 / 4.25)
    for _ in range(9):
        approx = apply_left(approx, 2.0 * identity - apply_left(square, approx))
    return approx


def lower_inverse(gram):
    factor = jnp.linalg.cholesky(gram)
    identity = jnp.eye(gram.shape[0], dtype=jnp.float32)
    return lax.linalg.triangular_solve(factor, identity, left_side=True, lower=True)


def make_local(rows_size):
    def local(matrix):
        block_count, width, local_rows = matrix.shape
        current = matrix.reshape(block_count * width, local_rows)
        global_rows = lax.axis_index("rows") * local_rows + jnp.arange(local_rows, dtype=jnp.int32)
        identity = jnp.eye(width, dtype=jnp.float32)
        lanes = jnp.arange(width, dtype=jnp.int32)[:, None]
        units = [
            (lanes == (global_rows - k * width)[None, :]).astype(jnp.float32) for k in range(2)
        ]

        gathered = lax.all_gather(current, "cols")
        panel_0 = gathered[0]
        second = gathered[1]

        sums = jnp.stack([
            inner_rows(panel_0, panel_0),
            inner_rows(panel_0, units[0]),
            inner_rows(panel_0, current),
            inner_rows(units[0], current),
            inner_rows(panel_0, second),
            inner_rows(units[0], second),
        ])
        sums = butterfly_sum(sums, "rows", rows_size)
        gram, top_rows, basis_cur, unit_cur, basis_sec, unit_sec = (sums[i] for i in range(6))
        lower_inv = lower_inverse(gram)
        top_block = apply_left(lower_inv, top_rows)
        inverse = invert_near_identity(identity - top_block.T)
        reflect = units[0] - apply_left(lower_inv, panel_0)
        mixed = apply_left(inverse, unit_cur - apply_left(lower_inv, basis_cur))
        mixed_sec = apply_left(inverse, unit_sec - apply_left(lower_inv, basis_sec))
        current = current - jnp.dot(mixed.T, reflect, precision=HIGHEST_PRECISION)
        second = second - jnp.dot(mixed_sec.T, reflect, precision=HIGHEST_PRECISION)

        panel_1 = jnp.where((global_rows >= width)[None, :], second, jnp.zeros_like(second))
        sums = jnp.stack([
            inner_rows(panel_1, panel_1),
            inner_rows(panel_1, units[1]),
            inner_rows(panel_1, current),
            inner_rows(units[1], current),
        ])
        sums = butterfly_sum(sums, "rows", rows_size)
        gram, top_rows, basis_cur, unit_cur = (sums[i] for i in range(4))
        lower_inv = lower_inverse(gram)
        top_block = apply_left(lower_inv, top_rows)
        inverse = invert_near_identity(identity - top_block.T)
        reflect = units[1] - apply_left(lower_inv, panel_1)
        mixed = apply_left(inverse, unit_cur - apply_left(lower_inv, basis_cur))
        current = current - jnp.dot(mixed.T, reflect, precision=HIGHEST_PRECISION)
        return current.reshape(matrix.shape)

    return local


def solution(mesh):
    return jax.shard_map(
        make_local(mesh.shape["rows"]),
        mesh=mesh,
        in_specs=(P(None, "cols", "rows"),),
        out_specs=P(None, "cols", "rows"),
        check_vma=False,
    )
```

```python
import jax
import jax.numpy as jnp
from jax import lax
from jax.experimental import pallas as pl
from jax.sharding import PartitionSpec as P

HIGHEST_PRECISION = lax.Precision.HIGHEST


def inner_rows(left, right):
    return lax.dot_general(left, right, (((1,), (1,)), ((), ())), precision=HIGHEST_PRECISION)


def apply_left(square, right_side):
    return jnp.dot(square, right_side, precision=HIGHEST_PRECISION)


def butterfly_sum(x, axis, size):
    if size & (size - 1):
        return lax.psum(x, axis)
    step = 1
    while step < size:
        x = x + lax.ppermute(x, axis, [(i, i ^ step) for i in range(size)])
        step *= 2
    return x


def invert_near_identity(square):
    identity = jnp.eye(square.shape[0], dtype=jnp.float32)
    approx = square.T * (2.0 / 4.25)
    for _ in range(9):
        approx = apply_left(approx, 2.0 * identity - apply_left(square, approx))
    return approx


def _eliminate_kernel(aug_ref, out_ref):
    size, wide = aug_ref.shape
    rows = lax.broadcasted_iota(jnp.int32, (size, wide), 0)
    lanes = lax.broadcasted_iota(jnp.int32, (size, wide), 1)
    row_ids = lax.broadcasted_iota(jnp.int32, (size, 1), 0)

    def step(j, work):
        column = jnp.sum(jnp.where(lanes == j, work, 0.0), axis=1, keepdims=True)
        row = jnp.sum(jnp.where(rows == j, work, 0.0), axis=0, keepdims=True)
        pivot = jnp.sum(jnp.where(row_ids == j, column, 0.0), axis=0, keepdims=True)
        scale = 1.0 / jnp.sqrt(pivot)
        scaled = row * scale
        weight = jnp.where(row_ids > j, column * scale, 0.0)
        work = work - weight * scaled
        return jnp.where(rows == j, scaled, work)

    out_ref[...] = lax.fori_loop(0, size, step, aug_ref[...], unroll=4)


def lower_inverse(gram):
    size = gram.shape[0]
    aug = jnp.concatenate([gram, jnp.eye(size, dtype=jnp.float32)], axis=1)
    out = pl.pallas_call(
        _eliminate_kernel, out_shape=jax.ShapeDtypeStruct(aug.shape, jnp.float32)
    )(aug)
    return out[:, size:]


def make_local(rows_size):
    def local(matrix):
        block_count, width, local_rows = matrix.shape
        current = matrix.reshape(block_count * width, local_rows)
        global_rows = lax.axis_index("rows") * local_rows + jnp.arange(local_rows, dtype=jnp.int32)
        identity = jnp.eye(width, dtype=jnp.float32)
        lanes = jnp.arange(width, dtype=jnp.int32)[:, None]
        units = [
            (lanes == (global_rows - k * width)[None, :]).astype(jnp.float32) for k in range(2)
        ]

        gathered = lax.all_gather(current, "cols")
        panel_0 = gathered[0]
        second = gathered[1]

        sums = jnp.stack([
            inner_rows(panel_0, panel_0),
            inner_rows(panel_0, units[0]),
            inner_rows(panel_0, current),
            inner_rows(units[0], current),
            inner_rows(panel_0, second),
            inner_rows(units[0], second),
        ])
        sums = butterfly_sum(sums, "rows", rows_size)
        gram, top_rows, basis_cur, unit_cur, basis_sec, unit_sec = (sums[i] for i in range(6))
        lower_inv = lower_inverse(gram)
        top_block = apply_left(lower_inv, top_rows)
        inverse = invert_near_identity(identity - top_block.T)
        reflect = units[0] - apply_left(lower_inv, panel_0)
        mixed = apply_left(inverse, unit_cur - apply_left(lower_inv, basis_cur))
        mixed_sec = apply_left(inverse, unit_sec - apply_left(lower_inv, basis_sec))
        current = current - jnp.dot(mixed.T, reflect, precision=HIGHEST_PRECISION)
        second = second - jnp.dot(mixed_sec.T, reflect, precision=HIGHEST_PRECISION)

        panel_1 = jnp.where((global_rows >= width)[None, :], second, jnp.zeros_like(second))
        sums = jnp.stack([
            inner_rows(panel_1, panel_1),
            inner_rows(panel_1, units[1]),
            inner_rows(panel_1, current),
            inner_rows(units[1], current),
        ])
        sums = butterfly_sum(sums, "rows", rows_size)
        gram, top_rows, basis_cur, unit_cur = (sums[i] for i in range(4))
        lower_inv = lower_inverse(gram)
        top_block = apply_left(lower_inv, top_rows)
        inverse = invert_near_identity(identity - top_block.T)
        reflect = units[1] - apply_left(lower_inv, panel_1)
        mixed = apply_left(inverse, unit_cur - apply_left(lower_inv, basis_cur))
        current = current - jnp.dot(mixed.T, reflect, precision=HIGHEST_PRECISION)
        return current.reshape(matrix.shape)

    return local


def solution(mesh):
    return jax.shard_map(
        make_local(mesh.shape["rows"]),
        mesh=mesh,
        in_specs=(P(None, "cols", "rows"),),
        out_specs=P(None, "cols", "rows"),
        check_vma=False,
    )
```

```python
import jax
import jax.numpy as jnp
from jax import lax
from jax.experimental import pallas as pl
from jax.sharding import PartitionSpec as P

HIGHEST_PRECISION = lax.Precision.HIGHEST


def inner_rows(left, right):
    return lax.dot_general(left, right, (((1,), (1,)), ((), ())), precision=HIGHEST_PRECISION)


def apply_left(square, right_side):
    return jnp.dot(square, right_side, precision=HIGHEST_PRECISION)


def butterfly_sum(x, axis, size):
    if size & (size - 1):
        return lax.psum(x, axis)
    step = 1
    while step < size:
        x = x + lax.ppermute(x, axis, [(i, i ^ step) for i in range(size)])
        step *= 2
    return x


def invert_near_identity(square):
    identity = jnp.eye(square.shape[0], dtype=jnp.float32)
    approx = square.T * (2.0 / 4.25)
    for _ in range(8):
        approx = apply_left(approx, 2.0 * identity - apply_left(square, approx))
    return approx


def _eliminate_kernel(aug_ref, out_ref):
    size, wide = aug_ref.shape
    rows = lax.broadcasted_iota(jnp.int32, (size, wide), 0)
    lanes = lax.broadcasted_iota(jnp.int32, (size, wide), 1)
    row_ids = lax.broadcasted_iota(jnp.int32, (size, 1), 0)

    def step(j, work):
        column = jnp.sum(jnp.where(lanes == j, work, 0.0), axis=1, keepdims=True)
        row = jnp.sum(jnp.where(rows == j, work, 0.0), axis=0, keepdims=True)
        pivot = jnp.sum(jnp.where(row_ids == j, column, 0.0), axis=0, keepdims=True)
        scale = 1.0 / jnp.sqrt(pivot)
        scaled = row * scale
        weight = jnp.where(row_ids > j, column * scale, 0.0)
        work = work - weight * scaled
        return jnp.where(rows == j, scaled, work)

    out_ref[...] = lax.fori_loop(0, size, step, aug_ref[...], unroll=4)


def lower_inverse(gram):
    size = gram.shape[0]
    aug = jnp.concatenate([gram, jnp.eye(size, dtype=jnp.float32)], axis=1)
    out = pl.pallas_call(
        _eliminate_kernel, out_shape=jax.ShapeDtypeStruct(aug.shape, jnp.float32)
    )(aug)
    return out[:, size:]


def make_local(rows_size):
    def local(matrix):
        block_count, width, local_rows = matrix.shape
        current = matrix.reshape(block_count * width, local_rows)
        global_rows = lax.axis_index("rows") * local_rows + jnp.arange(local_rows, dtype=jnp.int32)
        identity = jnp.eye(width, dtype=jnp.float32)
        lanes = jnp.arange(width, dtype=jnp.int32)[:, None]
        units = [
            (lanes == (global_rows - k * width)[None, :]).astype(jnp.float32) for k in range(2)
        ]

        gathered = lax.all_gather(current, "cols")
        panel_0 = gathered[0]
        second = gathered[1]

        head = butterfly_sum(jnp.stack([
            inner_rows(panel_0, panel_0),
            inner_rows(panel_0, units[0]),
        ]), "rows", rows_size)
        tail = butterfly_sum(jnp.stack([
            inner_rows(panel_0, current),
            inner_rows(units[0], current),
            inner_rows(panel_0, second),
            inner_rows(units[0], second),
        ]), "rows", rows_size)
        gram, top_rows = head[0], head[1]
        basis_cur, unit_cur, basis_sec, unit_sec = (tail[i] for i in range(4))
        lower_inv = lower_inverse(gram)
        top_block = apply_left(lower_inv, top_rows)
        inverse = invert_near_identity(identity - top_block.T)
        reflect = units[0] - apply_left(lower_inv, panel_0)
        mixed = apply_left(inverse, unit_cur - apply_left(lower_inv, basis_cur))
        mixed_sec = apply_left(inverse, unit_sec - apply_left(lower_inv, basis_sec))
        current = current - jnp.dot(mixed.T, reflect, precision=HIGHEST_PRECISION)
        second = second - jnp.dot(mixed_sec.T, reflect, precision=HIGHEST_PRECISION)

        panel_1 = jnp.where((global_rows >= width)[None, :], second, jnp.zeros_like(second))
        head = butterfly_sum(jnp.stack([
            inner_rows(panel_1, panel_1),
            inner_rows(panel_1, units[1]),
        ]), "rows", rows_size)
        tail = butterfly_sum(jnp.stack([
            inner_rows(panel_1, current),
            inner_rows(units[1], current),
        ]), "rows", rows_size)
        gram, top_rows = head[0], head[1]
        basis_cur, unit_cur = tail[0], tail[1]
        lower_inv = lower_inverse(gram)
        top_block = apply_left(lower_inv, top_rows)
        inverse = invert_near_identity(identity - top_block.T)
        reflect = units[1] - apply_left(lower_inv, panel_1)
        mixed = apply_left(inverse, unit_cur - apply_left(lower_inv, basis_cur))
        current = current - jnp.dot(mixed.T, reflect, precision=HIGHEST_PRECISION)
        return current.reshape(matrix.shape)

    return local


def solution(mesh):
    return jax.shard_map(
        make_local(mesh.shape["rows"]),
        mesh=mesh,
        in_specs=(P(None, "cols", "rows"),),
        out_specs=P(None, "cols", "rows"),
        check_vma=False,
    )
```

```python
import jax
import jax.numpy as jnp
from jax import lax
from jax.experimental import pallas as pl
from jax.sharding import PartitionSpec as P

HIGHEST_PRECISION = lax.Precision.HIGHEST


def inner_rows(left, right):
    return lax.dot_general(left, right, (((1,), (1,)), ((), ())), precision=HIGHEST_PRECISION)


def apply_left(square, right_side):
    return jnp.dot(square, right_side, precision=HIGHEST_PRECISION)


def butterfly_sum(x, axis, size):
    if size & (size - 1):
        return lax.psum(x, axis)
    step = 1
    while step < size:
        x = x + lax.ppermute(x, axis, [(i, i ^ step) for i in range(size)])
        step *= 2
    return x


def invert_near_identity(square):
    identity = jnp.eye(square.shape[0], dtype=jnp.float32)
    approx = square.T * (2.0 / 4.25)
    for _ in range(8):
        approx = apply_left(approx, 2.0 * identity - apply_left(square, approx))
    return approx


def _eliminate_kernel(aug_ref, out_ref):
    size, wide = aug_ref.shape
    rows = lax.broadcasted_iota(jnp.int32, (size, wide), 0)
    lanes = lax.broadcasted_iota(jnp.int32, (size, wide), 1)
    row_ids = lax.broadcasted_iota(jnp.int32, (size, 1), 0)

    def step(j, work):
        column = jnp.sum(jnp.where(lanes == j, work, 0.0), axis=1, keepdims=True)
        row = jnp.sum(jnp.where(rows == j, work, 0.0), axis=0, keepdims=True)
        pivot = jnp.sum(jnp.where(row_ids == j, column, 0.0), axis=0, keepdims=True)
        scale = 1.0 / jnp.sqrt(pivot)
        scaled = row * scale
        weight = jnp.where(row_ids > j, column * scale, 0.0)
        work = work - weight * scaled
        return jnp.where(rows == j, scaled, work)

    out_ref[...] = lax.fori_loop(0, size, step, aug_ref[...], unroll=4)


def lower_inverse(gram):
    size = gram.shape[0]
    aug = jnp.concatenate([gram, jnp.eye(size, dtype=jnp.float32)], axis=1)
    out = pl.pallas_call(
        _eliminate_kernel, out_shape=jax.ShapeDtypeStruct(aug.shape, jnp.float32)
    )(aug)
    return out[:, size:]


def make_local(rows_size):
    def local(matrix):
        block_count, width, local_rows = matrix.shape
        current = matrix.reshape(block_count * width, local_rows)
        global_rows = lax.axis_index("rows") * local_rows + jnp.arange(local_rows, dtype=jnp.int32)
        identity = jnp.eye(width, dtype=jnp.float32)
        lanes = jnp.arange(width, dtype=jnp.int32)[:, None]
        units = [
            (lanes == (global_rows - k * width)[None, :]).astype(jnp.float32) for k in range(2)
        ]

        gathered = lax.all_gather(current, "cols")
        panel_0 = gathered[0]
        second = gathered[1]

        def reduce_rows(*pairs):
            return butterfly_sum(
                jnp.stack([inner_rows(a, b) for a, b in pairs]), "rows", rows_size
            )

        gram = reduce_rows((panel_0, panel_0))[0]
        tail = reduce_rows((panel_0, units[0]), (panel_0, second), (units[0], second))
        late = reduce_rows((panel_0, current), (units[0], current))
        lower_inv = lower_inverse(gram)
        top_block = apply_left(lower_inv, tail[0])
        inverse = invert_near_identity(identity - top_block.T)
        reflect = units[0] - apply_left(lower_inv, panel_0)
        mixed_sec = apply_left(inverse, tail[2] - apply_left(lower_inv, tail[1]))
        second = second - jnp.dot(mixed_sec.T, reflect, precision=HIGHEST_PRECISION)

        panel_1 = jnp.where((global_rows >= width)[None, :], second, jnp.zeros_like(second))
        gram_1 = reduce_rows((panel_1, panel_1))[0]
        tail_1 = reduce_rows(
            (panel_1, units[1]),
            (panel_1, current),
            (units[1], current),
            (panel_1, panel_0),
            (units[1], panel_0),
        )
        mixed = apply_left(inverse, late[1] - apply_left(lower_inv, late[0]))
        back = jnp.dot(lower_inv.T, mixed, precision=HIGHEST_PRECISION)
        basis_cur = tail_1[1] + apply_left(tail_1[3], back)
        unit_cur = tail_1[2] + apply_left(tail_1[4], back)
        lower_inv_1 = lower_inverse(gram_1)
        top_block = apply_left(lower_inv_1, tail_1[0])
        inverse_1 = invert_near_identity(identity - top_block.T)
        reflect_1 = units[1] - apply_left(lower_inv_1, panel_1)
        mixed_1 = apply_left(inverse_1, unit_cur - apply_left(lower_inv_1, basis_cur))
        current = current - jnp.dot(mixed.T, reflect, precision=HIGHEST_PRECISION)
        current = current - jnp.dot(mixed_1.T, reflect_1, precision=HIGHEST_PRECISION)
        return current.reshape(matrix.shape)

    return local


def solution(mesh):
    return jax.shard_map(
        make_local(mesh.shape["rows"]),
        mesh=mesh,
        in_specs=(P(None, "cols", "rows"),),
        out_specs=P(None, "cols", "rows"),
        check_vma=False,
    )
```

```python
import jax
import jax.numpy as jnp
from jax import lax
from jax.experimental import pallas as pl
from jax.sharding import PartitionSpec as P

HIGHEST_PRECISION = lax.Precision.HIGHEST


def inner_rows(left, right):
    return lax.dot_general(left, right, (((1,), (1,)), ((), ())), precision=HIGHEST_PRECISION)


def apply_left(square, right_side):
    return jnp.dot(square, right_side, precision=HIGHEST_PRECISION)


def butterfly_sum(x, axis, size):
    if size & (size - 1):
        return lax.psum(x, axis)
    step = 1
    while step < size:
        x = x + lax.ppermute(x, axis, [(i, i ^ step) for i in range(size)])
        step *= 2
    return x


def paired_sums(head, tail, axis, size):
    if size & (size - 1) or size < 2:
        return lax.psum(head, axis), lax.psum(tail, axis)
    step = 1
    while step < size:
        head = head + lax.ppermute(head, axis, [(i, i ^ step) for i in range(size)])
        if 2 * step < size:
            tail = tail + lax.ppermute(tail, axis, [(i, i ^ step) for i in range(size)])
            head, tail = lax.optimization_barrier((head, tail))
        step *= 2
    step //= 2
    tail = tail + lax.ppermute(tail, axis, [(i, i ^ step) for i in range(size)])
    return head, tail


def invert_near_identity(square):
    identity = jnp.eye(square.shape[0], dtype=jnp.float32)
    approx = square.T * (2.0 / 4.25)
    for _ in range(8):
        approx = apply_left(approx, 2.0 * identity - apply_left(square, approx))
    return approx


def _eliminate_kernel(aug_ref, out_ref):
    size, wide = aug_ref.shape
    rows = lax.broadcasted_iota(jnp.int32, (size, wide), 0)
    lanes = lax.broadcasted_iota(jnp.int32, (size, wide), 1)
    row_ids = lax.broadcasted_iota(jnp.int32, (size, 1), 0)

    def step(j, work):
        column = jnp.sum(jnp.where(lanes == j, work, 0.0), axis=1, keepdims=True)
        row = jnp.sum(jnp.where(rows == j, work, 0.0), axis=0, keepdims=True)
        pivot = jnp.sum(jnp.where(row_ids == j, column, 0.0), axis=0, keepdims=True)
        scale = 1.0 / jnp.sqrt(pivot)
        scaled = row * scale
        weight = jnp.where(row_ids > j, column * scale, 0.0)
        work = work - weight * scaled
        return jnp.where(rows == j, scaled, work)

    out_ref[...] = lax.fori_loop(0, size, step, aug_ref[...], unroll=4)


def lower_inverse(gram):
    size = gram.shape[0]
    aug = jnp.concatenate([gram, jnp.eye(size, dtype=jnp.float32)], axis=1)
    out = pl.pallas_call(
        _eliminate_kernel, out_shape=jax.ShapeDtypeStruct(aug.shape, jnp.float32)
    )(aug)
    return out[:, size:]


def make_local(rows_size):
    def local(matrix):
        block_count, width, local_rows = matrix.shape
        current = matrix.reshape(block_count * width, local_rows)
        global_rows = lax.axis_index("rows") * local_rows + jnp.arange(local_rows, dtype=jnp.int32)
        identity = jnp.eye(width, dtype=jnp.float32)
        lanes = jnp.arange(width, dtype=jnp.int32)[:, None]
        units = [
            (lanes == (global_rows - k * width)[None, :]).astype(jnp.float32) for k in range(2)
        ]

        gathered = lax.all_gather(current, "cols")
        panel_0 = gathered[0]
        second = gathered[1]

        head, tail = paired_sums(
            jnp.stack([inner_rows(panel_0, panel_0), inner_rows(panel_0, units[0])]),
            jnp.stack([
                inner_rows(panel_0, current),
                inner_rows(units[0], current),
                inner_rows(panel_0, second),
                inner_rows(units[0], second),
            ]),
            "rows",
            rows_size,
        )
        gram, top_rows = head[0], head[1]
        basis_cur, unit_cur, basis_sec, unit_sec = (tail[i] for i in range(4))
        lower_inv = lower_inverse(gram)
        top_block = apply_left(lower_inv, top_rows)
        inverse = invert_near_identity(identity - top_block.T)
        reflect = units[0] - apply_left(lower_inv, panel_0)
        mixed = apply_left(inverse, unit_cur - apply_left(lower_inv, basis_cur))
        mixed_sec = apply_left(inverse, unit_sec - apply_left(lower_inv, basis_sec))
        current = current - jnp.dot(mixed.T, reflect, precision=HIGHEST_PRECISION)
        second = second - jnp.dot(mixed_sec.T, reflect, precision=HIGHEST_PRECISION)

        panel_1 = jnp.where((global_rows >= width)[None, :], second, jnp.zeros_like(second))
        head, tail = paired_sums(
            jnp.stack([inner_rows(panel_1, panel_1), inner_rows(panel_1, units[1])]),
            jnp.stack([inner_rows(panel_1, current), inner_rows(units[1], current)]),
            "rows",
            rows_size,
        )
        gram, top_rows = head[0], head[1]
        basis_cur, unit_cur = tail[0], tail[1]
        lower_inv = lower_inverse(gram)
        top_block = apply_left(lower_inv, top_rows)
        inverse = invert_near_identity(identity - top_block.T)
        reflect = units[1] - apply_left(lower_inv, panel_1)
        mixed = apply_left(inverse, unit_cur - apply_left(lower_inv, basis_cur))
        current = current - jnp.dot(mixed.T, reflect, precision=HIGHEST_PRECISION)
        return current.reshape(matrix.shape)

    return local


def solution(mesh):
    return jax.shard_map(
        make_local(mesh.shape["rows"]),
        mesh=mesh,
        in_specs=(P(None, "cols", "rows"),),
        out_specs=P(None, "cols", "rows"),
        check_vma=False,
    )
```

```python
import jax
import jax.numpy as jnp
from jax import lax
from jax.experimental import pallas as pl
from jax.sharding import PartitionSpec as P

HIGHEST_PRECISION = lax.Precision.HIGHEST


def inner_rows(left, right):
    return lax.dot_general(left, right, (((1,), (1,)), ((), ())), precision=HIGHEST_PRECISION)


def apply_left(square, right_side):
    return jnp.dot(square, right_side, precision=HIGHEST_PRECISION)


def butterfly_sum(x, axis, size):
    if size & (size - 1):
        return lax.psum(x, axis)
    step = 1
    while step < size:
        x = x + lax.ppermute(x, axis, [(i, i ^ step) for i in range(size)])
        step *= 2
    return x


def invert_near_identity(square):
    identity = jnp.eye(square.shape[0], dtype=jnp.float32)
    approx = square.T * (2.0 / 4.25)
    for _ in range(8):
        approx = apply_left(approx, 2.0 * identity - apply_left(square, approx))
    return approx


def _eliminate_kernel(aug_ref, out_ref):
    size, wide = aug_ref.shape
    rows = lax.broadcasted_iota(jnp.int32, (size, wide), 0)
    lanes = lax.broadcasted_iota(jnp.int32, (size, wide), 1)
    row_ids = lax.broadcasted_iota(jnp.int32, (size, 1), 0)

    def step(j, work):
        column = jnp.sum(jnp.where(lanes == j, work, 0.0), axis=1, keepdims=True)
        row = jnp.sum(jnp.where(rows == j, work, 0.0), axis=0, keepdims=True)
        pivot = jnp.sum(jnp.where(row_ids == j, column, 0.0), axis=0, keepdims=True)
        scale = 1.0 / jnp.sqrt(pivot)
        scaled = row * scale
        weight = jnp.where(row_ids > j, column * scale, 0.0)
        work = work - weight * scaled
        return jnp.where(rows == j, scaled, work)

    out_ref[...] = lax.fori_loop(0, size, step, aug_ref[...], unroll=4)


def lower_inverse(gram):
    size = gram.shape[0]
    aug = jnp.concatenate([gram, jnp.eye(size, dtype=jnp.float32)], axis=1)
    out = pl.pallas_call(
        _eliminate_kernel, out_shape=jax.ShapeDtypeStruct(aug.shape, jnp.float32)
    )(aug)
    return out[:, size:]


def make_local(rows_size):
    def local(matrix):
        block_count, width, local_rows = matrix.shape
        current = matrix.reshape(block_count * width, local_rows)
        global_rows = lax.axis_index("rows") * local_rows + jnp.arange(local_rows, dtype=jnp.int32)
        identity = jnp.eye(width, dtype=jnp.float32)
        lanes = jnp.arange(width, dtype=jnp.int32)[:, None]
        units = [
            (lanes == (global_rows - k * width)[None, :]).astype(jnp.float32) for k in range(2)
        ]

        gathered = lax.all_gather(current, "cols")
        panel_0 = gathered[0]
        second = gathered[1]

        head = butterfly_sum(
            inner_rows(panel_0, jnp.concatenate([panel_0, units[0]])), "rows", rows_size
        )
        both = jnp.concatenate([current, second])
        tail = butterfly_sum(
            jnp.concatenate([inner_rows(panel_0, both), inner_rows(units[0], both)], axis=1),
            "rows",
            rows_size,
        )
        gram, top_rows = head[:, :width], head[:, width:]
        basis_cur, basis_sec, unit_cur, unit_sec = (
            tail[:, i * width:(i + 1) * width] for i in range(4)
        )
        lower_inv = lower_inverse(gram)
        top_block = apply_left(lower_inv, top_rows)
        inverse = invert_near_identity(identity - top_block.T)
        reflect = units[0] - apply_left(lower_inv, panel_0)
        mixed = apply_left(inverse, unit_cur - apply_left(lower_inv, basis_cur))
        mixed_sec = apply_left(inverse, unit_sec - apply_left(lower_inv, basis_sec))
        current = current - jnp.dot(mixed.T, reflect, precision=HIGHEST_PRECISION)
        second = second - jnp.dot(mixed_sec.T, reflect, precision=HIGHEST_PRECISION)

        panel_1 = jnp.where((global_rows >= width)[None, :], second, jnp.zeros_like(second))
        head = butterfly_sum(
            inner_rows(panel_1, jnp.concatenate([panel_1, units[1]])), "rows", rows_size
        )
        tail = butterfly_sum(
            jnp.concatenate([inner_rows(panel_1, current), inner_rows(units[1], current)], axis=1),
            "rows",
            rows_size,
        )
        gram, top_rows = head[:, :width], head[:, width:]
        basis_cur, unit_cur = tail[:, :width], tail[:, width:]
        lower_inv = lower_inverse(gram)
        top_block = apply_left(lower_inv, top_rows)
        inverse = invert_near_identity(identity - top_block.T)
        reflect = units[1] - apply_left(lower_inv, panel_1)
        mixed = apply_left(inverse, unit_cur - apply_left(lower_inv, basis_cur))
        current = current - jnp.dot(mixed.T, reflect, precision=HIGHEST_PRECISION)
        return current.reshape(matrix.shape)

    return local


def solution(mesh):
    return jax.shard_map(
        make_local(mesh.shape["rows"]),
        mesh=mesh,
        in_specs=(P(None, "cols", "rows"),),
        out_specs=P(None, "cols", "rows"),
        check_vma=False,
    )
```

```python
import jax
import jax.numpy as jnp
from jax import lax
from jax.experimental import pallas as pl
from jax.sharding import PartitionSpec as P

HIGHEST_PRECISION = lax.Precision.HIGHEST


def inner_rows(left, right):
    return lax.dot_general(left, right, (((1,), (1,)), ((), ())), precision=HIGHEST_PRECISION)


def apply_left(square, right_side):
    return jnp.dot(square, right_side, precision=HIGHEST_PRECISION)


def butterfly_steps(size):
    if size < 2 or size & (size - 1):
        return None
    return [1 << k for k in range(size.bit_length() - 1)]


def butterfly_sum(x, axis, size, steps=None):
    every = butterfly_steps(size)
    if every is None:
        return x if steps == [] else lax.psum(x, axis)
    for step in every if steps is None else steps:
        x = x + lax.ppermute(x, axis, [(i, i ^ step) for i in range(size)])
    return x


def invert_near_identity(square):
    identity = jnp.eye(square.shape[0], dtype=jnp.float32)
    approx = square.T * (2.0 / 4.25)
    for _ in range(8):
        approx = apply_left(approx, 2.0 * identity - apply_left(square, approx))
    return approx


def _eliminate_kernel(aug_ref, out_ref):
    size, wide = aug_ref.shape
    rows = lax.broadcasted_iota(jnp.int32, (size, wide), 0)
    row_ids = lax.broadcasted_iota(jnp.int32, (size, 1), 0)
    work = aug_ref[...]
    for j in range(size):
        row = work[j:j + 1, :]
        pivot = row[:, j:j + 1]
        scale = lax.rsqrt(pivot)
        scale = scale * (1.5 - 0.5 * pivot * scale * scale)
        scaled = row * scale
        weight = jnp.where(row_ids > j, work[:, j:j + 1] * scale, 0.0)
        work = jnp.where(rows == j, scaled, work - weight * scaled)
    out_ref[...] = work


def lower_inverse(gram):
    size = gram.shape[0]
    aug = jnp.concatenate([gram, jnp.eye(size, dtype=jnp.float32)], axis=1)
    out = pl.pallas_call(
        _eliminate_kernel, out_shape=jax.ShapeDtypeStruct(aug.shape, jnp.float32)
    )(aug)
    return out[:, size:]


def make_local(rows_size):
    def local(matrix):
        block_count, width, local_rows = matrix.shape
        current = matrix.reshape(block_count * width, local_rows)
        global_rows = lax.axis_index("rows") * local_rows + jnp.arange(local_rows, dtype=jnp.int32)
        identity = jnp.eye(width, dtype=jnp.float32)
        lanes = jnp.arange(width, dtype=jnp.int32)[:, None]
        units = [
            (lanes == (global_rows - k * width)[None, :]).astype(jnp.float32) for k in range(2)
        ]

        gathered = lax.all_gather(current, "cols")
        panel_0 = gathered[0]
        second = gathered[1]

        head = butterfly_sum(
            inner_rows(panel_0, jnp.concatenate([panel_0, units[0]])), "rows", rows_size
        )
        both = jnp.concatenate([current, second])
        tail = jnp.concatenate([inner_rows(panel_0, both), inner_rows(units[0], both)], axis=1)
        steps = butterfly_steps(rows_size)
        tail = butterfly_sum(tail, "rows", rows_size, None if steps is None else steps[:-1])
        lower_inv, tail = lax.optimization_barrier((lower_inverse(head[:, :width]), tail))
        tail = butterfly_sum(tail, "rows", rows_size, None if steps is None else steps[-1:])
        top_rows = head[:, width:]
        basis_cur, basis_sec, unit_cur, unit_sec = (
            tail[:, i * width:(i + 1) * width] for i in range(4)
        )
        top_block = apply_left(lower_inv, top_rows)
        inverse = invert_near_identity(identity - top_block.T)
        reflect = units[0] - apply_left(lower_inv, panel_0)
        mixed = apply_left(inverse, unit_cur - apply_left(lower_inv, basis_cur))
        mixed_sec = apply_left(inverse, unit_sec - apply_left(lower_inv, basis_sec))
        current = current - jnp.dot(mixed.T, reflect, precision=HIGHEST_PRECISION)
        second = second - jnp.dot(mixed_sec.T, reflect, precision=HIGHEST_PRECISION)

        panel_1 = jnp.where((global_rows >= width)[None, :], second, jnp.zeros_like(second))
        head = butterfly_sum(
            inner_rows(panel_1, jnp.concatenate([panel_1, units[1]])), "rows", rows_size
        )
        tail = butterfly_sum(
            jnp.concatenate([inner_rows(panel_1, current), inner_rows(units[1], current)], axis=1),
            "rows",
            rows_size,
        )
        gram, top_rows = head[:, :width], head[:, width:]
        basis_cur, unit_cur = tail[:, :width], tail[:, width:]
        lower_inv = lower_inverse(gram)
        top_block = apply_left(lower_inv, top_rows)
        inverse = invert_near_identity(identity - top_block.T)
        reflect = units[1] - apply_left(lower_inv, panel_1)
        mixed = apply_left(inverse, unit_cur - apply_left(lower_inv, basis_cur))
        current = current - jnp.dot(mixed.T, reflect, precision=HIGHEST_PRECISION)
        return current.reshape(matrix.shape)

    return local


def solution(mesh):
    return jax.shard_map(
        make_local(mesh.shape["rows"]),
        mesh=mesh,
        in_specs=(P(None, "cols", "rows"),),
        out_specs=P(None, "cols", "rows"),
        check_vma=False,
    )
```

```python
import jax
import jax.numpy as jnp
from jax import lax
from jax.experimental import pallas as pl
from jax.sharding import PartitionSpec as P

HIGHEST_PRECISION = lax.Precision.HIGHEST


def inner_rows(left, right):
    return lax.dot_general(left, right, (((1,), (1,)), ((), ())), precision=HIGHEST_PRECISION)


def apply_left(square, right_side):
    return jnp.dot(square, right_side, precision=HIGHEST_PRECISION)


def butterfly_steps(size):
    if size < 2 or size & (size - 1):
        return None
    return [1 << k for k in range(size.bit_length() - 1)]


def butterfly_sum(x, axis, size, steps=None):
    every = butterfly_steps(size)
    if every is None:
        return x if steps == [] else lax.psum(x, axis)
    for step in every if steps is None else steps:
        x = x + lax.ppermute(x, axis, [(i, i ^ step) for i in range(size)])
    return x


def invert_near_identity(square):
    identity = jnp.eye(square.shape[0], dtype=jnp.float32)
    approx = square.T * (2.0 / 4.25)
    for _ in range(8):
        approx = apply_left(approx, 2.0 * identity - apply_left(square, approx))
    return approx


def _eliminate_kernel(head_ref, out_ref):
    size = out_ref.shape[0]
    wide = 2 * size
    rows = lax.broadcasted_iota(jnp.int32, (size, wide), 0)
    lanes = lax.broadcasted_iota(jnp.int32, (size, wide), 1)
    row_ids = lax.broadcasted_iota(jnp.int32, (size, 1), 0)
    work = head_ref[:, :wide]
    work = jnp.where(lanes < size, work, (lanes == rows + size).astype(jnp.float32))
    for j in range(size):
        row = work[j:j + 1, :]
        pivot = row[:, j:j + 1]
        scale = lax.rsqrt(pivot)
        scale = scale * (1.5 - 0.5 * pivot * scale * scale)
        scaled = row * scale
        weight = jnp.where(row_ids > j, work[:, j:j + 1] * scale, 0.0)
        work = jnp.where(rows == j, scaled, work - weight * scaled)
    out_ref[...] = work[:, size:]


def lower_inverse(head):
    size = head.shape[0]
    return pl.pallas_call(
        _eliminate_kernel, out_shape=jax.ShapeDtypeStruct((size, size), jnp.float32)
    )(head)


def make_local(rows_size):
    def local(matrix):
        block_count, width, local_rows = matrix.shape
        current = matrix.reshape(block_count * width, local_rows)
        global_rows = lax.axis_index("rows") * local_rows + jnp.arange(local_rows, dtype=jnp.int32)
        identity = jnp.eye(width, dtype=jnp.float32)
        lanes = jnp.arange(width, dtype=jnp.int32)[:, None]
        units = [
            (lanes == (global_rows - k * width)[None, :]).astype(jnp.float32) for k in range(2)
        ]

        gathered = lax.all_gather(current, "cols")
        panel_0 = gathered[0]
        second = gathered[1]

        head = butterfly_sum(
            inner_rows(panel_0, jnp.concatenate([panel_0, units[0]])), "rows", rows_size
        )
        both = jnp.concatenate([current, second])
        tail = jnp.concatenate([inner_rows(panel_0, both), inner_rows(units[0], both)], axis=1)
        steps = butterfly_steps(rows_size)
        tail = butterfly_sum(tail, "rows", rows_size, None if steps is None else steps[:-1])
        lower_inv, tail = lax.optimization_barrier((lower_inverse(head), tail))
        tail = butterfly_sum(tail, "rows", rows_size, None if steps is None else steps[-1:])
        top_rows = head[:, width:]
        basis_cur, basis_sec, unit_cur, unit_sec = (
            tail[:, i * width:(i + 1) * width] for i in range(4)
        )
        top_block = apply_left(lower_inv, top_rows)
        inverse = invert_near_identity(identity - top_block.T)
        reflect = units[0] - apply_left(lower_inv, panel_0)
        mixed = apply_left(inverse, unit_cur - apply_left(lower_inv, basis_cur))
        mixed_sec = apply_left(inverse, unit_sec - apply_left(lower_inv, basis_sec))
        current = current - jnp.dot(mixed.T, reflect, precision=HIGHEST_PRECISION)
        second = second - jnp.dot(mixed_sec.T, reflect, precision=HIGHEST_PRECISION)

        panel_1 = jnp.where((global_rows >= width)[None, :], second, jnp.zeros_like(second))
        head = butterfly_sum(
            inner_rows(panel_1, jnp.concatenate([panel_1, units[1]])), "rows", rows_size
        )
        tail = butterfly_sum(
            jnp.concatenate([inner_rows(panel_1, current), inner_rows(units[1], current)], axis=1),
            "rows",
            rows_size,
        )
        top_rows = head[:, width:]
        basis_cur, unit_cur = tail[:, :width], tail[:, width:]
        lower_inv = lower_inverse(head)
        top_block = apply_left(lower_inv, top_rows)
        inverse = invert_near_identity(identity - top_block.T)
        reflect = units[1] - apply_left(lower_inv, panel_1)
        mixed = apply_left(inverse, unit_cur - apply_left(lower_inv, basis_cur))
        current = current - jnp.dot(mixed.T, reflect, precision=HIGHEST_PRECISION)
        return current.reshape(matrix.shape)

    return local


def solution(mesh):
    return jax.shard_map(
        make_local(mesh.shape["rows"]),
        mesh=mesh,
        in_specs=(P(None, "cols", "rows"),),
        out_specs=P(None, "cols", "rows"),
        check_vma=False,
    )
```

```python
import jax
import jax.numpy as jnp
from jax import lax
from jax.experimental import pallas as pl
from jax.sharding import PartitionSpec as P

HIGHEST_PRECISION = lax.Precision.HIGHEST


def inner_rows(left, right):
    return lax.dot_general(left, right, (((1,), (1,)), ((), ())), precision=HIGHEST_PRECISION)


def apply_left(square, right_side):
    return jnp.dot(square, right_side, precision=HIGHEST_PRECISION)


def butterfly_steps(size):
    if size < 2 or size & (size - 1):
        return None
    return [1 << k for k in range(size.bit_length() - 1)]


def butterfly_sum(x, axis, size, steps=None):
    every = butterfly_steps(size)
    if every is None:
        return x if steps == [] else lax.psum(x, axis)
    for step in every if steps is None else steps:
        x = x + lax.ppermute(x, axis, [(i, i ^ step) for i in range(size)])
    return x


def invert_near_identity(square):
    identity = jnp.eye(square.shape[0], dtype=jnp.float32)
    approx = square.T * (2.0 / 4.25)
    for _ in range(8):
        approx = apply_left(approx, 2.0 * identity - apply_left(square, approx))
    return approx


def _eliminate_kernel(head_ref, out_ref):
    size = out_ref.shape[0]
    wide = 2 * size
    rows = lax.broadcasted_iota(jnp.int32, (size, wide), 0)
    lanes = lax.broadcasted_iota(jnp.int32, (size, wide), 1)
    row_ids = lax.broadcasted_iota(jnp.int32, (size, 1), 0)
    work = head_ref[:, :wide]
    work = jnp.where(lanes < size, work, (lanes == rows + size).astype(jnp.float32))
    for j in range(size):
        row = work[j:j + 1, :]
        pivot = row[:, j:j + 1]
        scale = lax.rsqrt(pivot)
        scale = scale * (1.5 - 0.5 * pivot * scale * scale)
        scaled = row * scale
        weight = jnp.where(row_ids > j, work[:, j:j + 1] * scale, 0.0)
        work = jnp.where(rows == j, scaled, work - weight * scaled)
    out_ref[...] = work[:, size:]


def lower_inverse(head):
    size = head.shape[0]
    return pl.pallas_call(
        _eliminate_kernel, out_shape=jax.ShapeDtypeStruct((size, size), jnp.float32)
    )(head)


def spread_pair(block, axis, size):
    index = lax.axis_index(axis)
    have = block
    dist = size // 2
    while dist >= 2:
        got = lax.ppermute(
            have, axis, [(i, i + dist) for i in range(size) if i % (2 * dist) < 2]
        )
        have = jnp.where(index % (2 * dist) >= dist, got, have)
        dist //= 2
    other = lax.ppermute(have, axis, [(i, i ^ 1) for i in range(size)])
    even = index % 2 == 0
    return jnp.where(even, have, other), jnp.where(even, other, have)


def spread_root(value, axis, size):
    index = lax.axis_index(axis)
    dist = size // 2
    while dist >= 1:
        got = lax.ppermute(
            value, axis, [(i, i + dist) for i in range(size) if i % (2 * dist) == 0]
        )
        value = jnp.where(index % (2 * dist) == dist, got, value)
        dist //= 2
    return value


def make_local(rows_size, cols_size):
    def local(matrix):
        block_count, width, local_rows = matrix.shape
        current = matrix.reshape(block_count * width, local_rows)
        global_rows = lax.axis_index("rows") * local_rows + jnp.arange(local_rows, dtype=jnp.int32)
        identity = jnp.eye(width, dtype=jnp.float32)
        lanes = jnp.arange(width, dtype=jnp.int32)[:, None]
        units = [
            (lanes == (global_rows - k * width)[None, :]).astype(jnp.float32) for k in range(2)
        ]

        if butterfly_steps(cols_size) is None:
            gathered = lax.all_gather(current, "cols")
            panel_0 = gathered[0]
            second = gathered[1]
            head = butterfly_sum(
                inner_rows(panel_0, jnp.concatenate([panel_0, units[0]])), "rows", rows_size
            )
        else:
            head = butterfly_sum(
                inner_rows(current, jnp.concatenate([current, units[0]])), "rows", rows_size
            )
            panel_0, second = spread_pair(current, "cols", cols_size)
            head = spread_root(head, "cols", cols_size)

        both = jnp.concatenate([current, second])
        tail = jnp.concatenate([inner_rows(panel_0, both), inner_rows(units[0], both)], axis=1)
        steps = butterfly_steps(rows_size)
        tail = butterfly_sum(tail, "rows", rows_size, None if steps is None else steps[:-1])
        lower_inv, tail = lax.optimization_barrier((lower_inverse(head), tail))
        tail = butterfly_sum(tail, "rows", rows_size, None if steps is None else steps[-1:])
        top_rows = head[:, width:]
        basis_cur, basis_sec, unit_cur, unit_sec = (
            tail[:, i * width:(i + 1) * width] for i in range(4)
        )
        top_block = apply_left(lower_inv, top_rows)
        inverse = invert_near_identity(identity - top_block.T)
        reflect = units[0] - apply_left(lower_inv, panel_0)
        mixed = apply_left(inverse, unit_cur - apply_left(lower_inv, basis_cur))
        mixed_sec = apply_left(inverse, unit_sec - apply_left(lower_inv, basis_sec))
        current = current - jnp.dot(mixed.T, reflect, precision=HIGHEST_PRECISION)
        second = second - jnp.dot(mixed_sec.T, reflect, precision=HIGHEST_PRECISION)

        panel_1 = jnp.where((global_rows >= width)[None, :], second, jnp.zeros_like(second))
        head = butterfly_sum(
            inner_rows(panel_1, jnp.concatenate([panel_1, units[1]])), "rows", rows_size
        )
        tail = butterfly_sum(
            jnp.concatenate([inner_rows(panel_1, current), inner_rows(units[1], current)], axis=1),
            "rows",
            rows_size,
        )
        top_rows = head[:, width:]
        basis_cur, unit_cur = tail[:, :width], tail[:, width:]
        lower_inv = lower_inverse(head)
        top_block = apply_left(lower_inv, top_rows)
        inverse = invert_near_identity(identity - top_block.T)
        reflect = units[1] - apply_left(lower_inv, panel_1)
        mixed = apply_left(inverse, unit_cur - apply_left(lower_inv, basis_cur))
        current = current - jnp.dot(mixed.T, reflect, precision=HIGHEST_PRECISION)
        return current.reshape(matrix.shape)

    return local


def solution(mesh):
    return jax.shard_map(
        make_local(mesh.shape["rows"], mesh.shape["cols"]),
        mesh=mesh,
        in_specs=(P(None, "cols", "rows"),),
        out_specs=P(None, "cols", "rows"),
        check_vma=False,
    )
```

```python
import jax
import jax.numpy as jnp
from jax import lax
from jax.experimental import pallas as pl
from jax.sharding import PartitionSpec as P

HIGHEST_PRECISION = lax.Precision.HIGHEST


def inner_rows(left, right):
    return lax.dot_general(left, right, (((1,), (1,)), ((), ())), precision=HIGHEST_PRECISION)


def apply_left(square, right_side):
    return jnp.dot(square, right_side, precision=HIGHEST_PRECISION)


def butterfly_steps(size):
    if size < 2 or size & (size - 1):
        return None
    return [1 << k for k in range(size.bit_length() - 1)]


def butterfly_sum(x, axis, size, steps=None):
    every = butterfly_steps(size)
    if every is None:
        return x if steps == [] else lax.psum(x, axis)
    for step in every if steps is None else steps:
        x = x + lax.ppermute(x, axis, [(i, i ^ step) for i in range(size)])
    return x


def invert_near_identity(square):
    identity = jnp.eye(square.shape[0], dtype=jnp.float32)
    approx = square.T * (2.0 / 4.25)
    for _ in range(8):
        approx = apply_left(approx, 2.0 * identity - apply_left(square, approx))
    return approx


def _eliminate_kernel(head_ref, out_ref):
    size = out_ref.shape[0]
    wide = 2 * size
    rows = lax.broadcasted_iota(jnp.int32, (size, wide), 0)
    lanes = lax.broadcasted_iota(jnp.int32, (size, wide), 1)
    row_ids = lax.broadcasted_iota(jnp.int32, (size, 1), 0)
    work = head_ref[:, :wide]
    work = jnp.where(lanes < size, work, (lanes == rows + size).astype(jnp.float32))
    for j in range(size):
        row = work[j:j + 1, :]
        pivot = row[:, j:j + 1]
        scale = lax.rsqrt(pivot)
        scale = scale * (1.5 - 0.5 * pivot * scale * scale)
        scaled = row * scale
        weight = jnp.where(row_ids > j, work[:, j:j + 1] * scale, 0.0)
        work = jnp.where(rows == j, scaled, work - weight * scaled)
    out_ref[...] = work[:, size:]


def lower_inverse(head):
    size = head.shape[0]
    return pl.pallas_call(
        _eliminate_kernel, out_shape=jax.ShapeDtypeStruct((size, size), jnp.float32)
    )(head)


def spread_pair(block, axis, size):
    index = lax.axis_index(axis)
    have = block
    dist = size // 2
    while dist >= 2:
        got = lax.ppermute(
            have, axis, [(i, i + dist) for i in range(size) if i % (2 * dist) < 2]
        )
        have = jnp.where(index % (2 * dist) >= dist, got, have)
        dist //= 2
    other = lax.ppermute(have, axis, [(i, i ^ 1) for i in range(size)])
    even = index % 2 == 0
    return jnp.where(even, have, other), jnp.where(even, other, have)


def from_root(value, axis, size):
    index = lax.axis_index(axis)
    for k in range(1, size):
        got = lax.ppermute(value, axis, [(0, k)])
        value = jnp.where(index == k, got, value)
    return value


def make_local(rows_size, cols_size):
    def local(matrix):
        block_count, width, local_rows = matrix.shape
        current = matrix.reshape(block_count * width, local_rows)
        global_rows = lax.axis_index("rows") * local_rows + jnp.arange(local_rows, dtype=jnp.int32)
        identity = jnp.eye(width, dtype=jnp.float32)
        lanes = jnp.arange(width, dtype=jnp.int32)[:, None]
        units = [
            (lanes == (global_rows - k * width)[None, :]).astype(jnp.float32) for k in range(2)
        ]

        if butterfly_steps(cols_size) is None:
            gathered = lax.all_gather(current, "cols")
            panel_0 = gathered[0]
            second = gathered[1]
            head = butterfly_sum(
                inner_rows(panel_0, jnp.concatenate([panel_0, units[0]])), "rows", rows_size
            )
        else:
            head = inner_rows(current, jnp.concatenate([current, units[0]]))
            head = butterfly_sum(from_root(head, "cols", cols_size), "rows", rows_size)
            panel_0, second = spread_pair(current, "cols", cols_size)

        both = jnp.concatenate([current, second])
        tail = jnp.concatenate([inner_rows(panel_0, both), inner_rows(units[0], both)], axis=1)
        steps = butterfly_steps(rows_size)
        tail = butterfly_sum(tail, "rows", rows_size, None if steps is None else steps[:-1])
        lower_inv, tail = lax.optimization_barrier((lower_inverse(head), tail))
        tail = butterfly_sum(tail, "rows", rows_size, None if steps is None else steps[-1:])
        top_rows = head[:, width:]
        basis_cur, basis_sec, unit_cur, unit_sec = (
            tail[:, i * width:(i + 1) * width] for i in range(4)
        )
        top_block = apply_left(lower_inv, top_rows)
        inverse = invert_near_identity(identity - top_block.T)
        reflect = units[0] - apply_left(lower_inv, panel_0)
        mixed = apply_left(inverse, unit_cur - apply_left(lower_inv, basis_cur))
        mixed_sec = apply_left(inverse, unit_sec - apply_left(lower_inv, basis_sec))
        current = current - jnp.dot(mixed.T, reflect, precision=HIGHEST_PRECISION)
        second = second - jnp.dot(mixed_sec.T, reflect, precision=HIGHEST_PRECISION)

        panel_1 = jnp.where((global_rows >= width)[None, :], second, jnp.zeros_like(second))
        head = butterfly_sum(
            inner_rows(panel_1, jnp.concatenate([panel_1, units[1]])), "rows", rows_size
        )
        tail = butterfly_sum(
            jnp.concatenate([inner_rows(panel_1, current), inner_rows(units[1], current)], axis=1),
            "rows",
            rows_size,
        )
        top_rows = head[:, width:]
        basis_cur, unit_cur = tail[:, :width], tail[:, width:]
        lower_inv = lower_inverse(head)
        top_block = apply_left(lower_inv, top_rows)
        inverse = invert_near_identity(identity - top_block.T)
        reflect = units[1] - apply_left(lower_inv, panel_1)
        mixed = apply_left(inverse, unit_cur - apply_left(lower_inv, basis_cur))
        current = current - jnp.dot(mixed.T, reflect, precision=HIGHEST_PRECISION)
        return current.reshape(matrix.shape)

    return local


def solution(mesh):
    return jax.shard_map(
        make_local(mesh.shape["rows"], mesh.shape["cols"]),
        mesh=mesh,
        in_specs=(P(None, "cols", "rows"),),
        out_specs=P(None, "cols", "rows"),
        check_vma=False,
    )
```

```python
import jax
import jax.numpy as jnp
from jax import lax
from jax.experimental import pallas as pl
from jax.sharding import PartitionSpec as P

HIGHEST_PRECISION = lax.Precision.HIGHEST


def inner_rows(left, right):
    return lax.dot_general(left, right, (((1,), (1,)), ((), ())), precision=HIGHEST_PRECISION)


def apply_left(square, right_side):
    return jnp.dot(square, right_side, precision=HIGHEST_PRECISION)


def butterfly_steps(size):
    if size < 2 or size & (size - 1):
        return None
    return [1 << k for k in range(size.bit_length() - 1)]


def butterfly_sum(x, axis, size, steps=None):
    every = butterfly_steps(size)
    if every is None:
        return x if steps == [] else lax.psum(x, axis)
    for step in every if steps is None else steps:
        x = x + lax.ppermute(x, axis, [(i, i ^ step) for i in range(size)])
    return x


def _eliminate_kernel(head_ref, lower_ref, inverse_ref):
    size = lower_ref.shape[0]
    wide = 2 * size
    rows = lax.broadcasted_iota(jnp.int32, (size, wide), 0)
    lanes = lax.broadcasted_iota(jnp.int32, (size, wide), 1)
    row_ids = lax.broadcasted_iota(jnp.int32, (size, 1), 0)
    head = head_ref[...]
    work = jnp.where(lanes < size, head, (lanes == rows + size).astype(jnp.float32))
    for j in range(size):
        row = work[j:j + 1, :]
        pivot = row[:, j:j + 1]
        scale = lax.rsqrt(pivot)
        scale = scale * (1.5 - 0.5 * pivot * scale * scale)
        scaled = row * scale
        weight = jnp.where(row_ids > j, work[:, j:j + 1] * scale, 0.0)
        work = jnp.where(rows == j, scaled, work - weight * scaled)
    lower_inv = work[:, size:]
    lower_ref[...] = lower_inv

    def dot(a, b):
        return jnp.dot(a, b, precision=HIGHEST_PRECISION, preferred_element_type=jnp.float32)

    identity = (rows[:, :size] == lanes[:, :size]).astype(jnp.float32)
    top_block = dot(lower_inv, head[:, size:])
    square = identity - top_block.T
    approx = square.T * (2.0 / 4.25)
    for _ in range(8):
        approx = dot(approx, 2.0 * identity - dot(square, approx))
    inverse_ref[...] = approx


def factor_and_inverse(head):
    size = head.shape[0]
    square = jax.ShapeDtypeStruct((size, size), jnp.float32)
    return pl.pallas_call(_eliminate_kernel, out_shape=(square, square))(head)


def spread_pair(block, axis, size):
    index = lax.axis_index(axis)
    have = block
    dist = size // 2
    while dist >= 2:
        got = lax.ppermute(
            have, axis, [(i, i + dist) for i in range(size) if i % (2 * dist) < 2]
        )
        have = jnp.where(index % (2 * dist) >= dist, got, have)
        dist //= 2
    other = lax.ppermute(have, axis, [(i, i ^ 1) for i in range(size)])
    even = index % 2 == 0
    return jnp.where(even, have, other), jnp.where(even, other, have)


def from_root(value, axis, size):
    index = lax.axis_index(axis)
    for k in range(1, size):
        got = lax.ppermute(value, axis, [(0, k)])
        value = jnp.where(index == k, got, value)
    return value


def make_local(rows_size, cols_size):
    def local(matrix):
        block_count, width, local_rows = matrix.shape
        current = matrix.reshape(block_count * width, local_rows)
        global_rows = lax.axis_index("rows") * local_rows + jnp.arange(local_rows, dtype=jnp.int32)
        lanes = jnp.arange(width, dtype=jnp.int32)[:, None]
        units = [
            (lanes == (global_rows - k * width)[None, :]).astype(jnp.float32) for k in range(2)
        ]

        if butterfly_steps(cols_size) is None:
            gathered = lax.all_gather(current, "cols")
            panel_0 = gathered[0]
            second = gathered[1]
            head = butterfly_sum(
                inner_rows(panel_0, jnp.concatenate([panel_0, units[0]])), "rows", rows_size
            )
        else:
            head = inner_rows(current, jnp.concatenate([current, units[0]]))
            head = butterfly_sum(from_root(head, "cols", cols_size), "rows", rows_size)
            panel_0, second = spread_pair(current, "cols", cols_size)

        both = jnp.concatenate([current, second])
        tail = jnp.concatenate([inner_rows(panel_0, both), inner_rows(units[0], both)], axis=1)
        steps = butterfly_steps(rows_size)
        tail = butterfly_sum(tail, "rows", rows_size, None if steps is None else steps[:-1])
        lower_inv, inverse, tail = lax.optimization_barrier((*factor_and_inverse(head), tail))
        tail = butterfly_sum(tail, "rows", rows_size, None if steps is None else steps[-1:])
        basis_cur, basis_sec, unit_cur, unit_sec = (
            tail[:, i * width:(i + 1) * width] for i in range(4)
        )
        reflect = units[0] - apply_left(lower_inv, panel_0)
        mixed = apply_left(inverse, unit_cur - apply_left(lower_inv, basis_cur))
        mixed_sec = apply_left(inverse, unit_sec - apply_left(lower_inv, basis_sec))
        current = current - jnp.dot(mixed.T, reflect, precision=HIGHEST_PRECISION)
        second = second - jnp.dot(mixed_sec.T, reflect, precision=HIGHEST_PRECISION)

        panel_1 = jnp.where((global_rows >= width)[None, :], second, jnp.zeros_like(second))
        head = butterfly_sum(
            inner_rows(panel_1, jnp.concatenate([panel_1, units[1]])), "rows", rows_size
        )
        tail = butterfly_sum(
            jnp.concatenate([inner_rows(panel_1, current), inner_rows(units[1], current)], axis=1),
            "rows",
            rows_size,
        )
        basis_cur, unit_cur = tail[:, :width], tail[:, width:]
        lower_inv, inverse = factor_and_inverse(head)
        reflect = units[1] - apply_left(lower_inv, panel_1)
        mixed = apply_left(inverse, unit_cur - apply_left(lower_inv, basis_cur))
        current = current - jnp.dot(mixed.T, reflect, precision=HIGHEST_PRECISION)
        return current.reshape(matrix.shape)

    return local


def solution(mesh):
    return jax.shard_map(
        make_local(mesh.shape["rows"], mesh.shape["cols"]),
        mesh=mesh,
        in_specs=(P(None, "cols", "rows"),),
        out_specs=P(None, "cols", "rows"),
        check_vma=False,
    )
```

```python
import jax
import jax.numpy as jnp
from jax import lax
from jax.experimental import pallas as pl
from jax.sharding import PartitionSpec as P

HIGHEST_PRECISION = lax.Precision.HIGHEST


def inner_rows(left, right):
    return lax.dot_general(left, right, (((1,), (1,)), ((), ())), precision=HIGHEST_PRECISION)


def apply_left(square, right_side):
    return jnp.dot(square, right_side, precision=HIGHEST_PRECISION)


def butterfly_steps(size):
    if size < 2 or size & (size - 1):
        return None
    return [1 << k for k in range(size.bit_length() - 1)]


def butterfly_sum(x, axis, size, steps=None):
    every = butterfly_steps(size)
    if every is None:
        return x if steps == [] else lax.psum(x, axis)
    for step in every if steps is None else steps:
        x = x + lax.ppermute(x, axis, [(i, i ^ step) for i in range(size)])
    return x


def invert_near_identity(square):
    identity = jnp.eye(square.shape[0], dtype=jnp.float32)
    approx = square.T * (2.0 / 4.25)
    for _ in range(7):
        approx = apply_left(approx, 2.0 * identity - apply_left(square, approx))
    return approx


def _eliminate_kernel(head_ref, out_ref):
    size = out_ref.shape[0]
    wide = 2 * size
    rows = lax.broadcasted_iota(jnp.int32, (size, wide), 0)
    lanes = lax.broadcasted_iota(jnp.int32, (size, wide), 1)
    row_ids = lax.broadcasted_iota(jnp.int32, (size, 1), 0)
    work = head_ref[:, :wide]
    work = jnp.where(lanes < size, work, (lanes == rows + size).astype(jnp.float32))
    for j in range(size):
        row = work[j:j + 1, :]
        pivot = row[:, j:j + 1]
        scale = lax.rsqrt(pivot)
        scale = scale * (1.5 - 0.5 * pivot * scale * scale)
        scaled = row * scale
        weight = jnp.where(row_ids > j, work[:, j:j + 1] * scale, 0.0)
        work = jnp.where(rows == j, scaled, work - weight * scaled)
    out_ref[...] = work[:, size:]


def lower_inverse(head):
    size = head.shape[0]
    return pl.pallas_call(
        _eliminate_kernel, out_shape=jax.ShapeDtypeStruct((size, size), jnp.float32)
    )(head)


def spread_pair(block, axis, size):
    index = lax.axis_index(axis)
    have = block
    dist = size // 2
    while dist >= 2:
        got = lax.ppermute(
            have, axis, [(i, i + dist) for i in range(size) if i % (2 * dist) < 2]
        )
        have = jnp.where(index % (2 * dist) >= dist, got, have)
        dist //= 2
    other = lax.ppermute(have, axis, [(i, i ^ 1) for i in range(size)])
    even = index % 2 == 0
    return jnp.where(even, have, other), jnp.where(even, other, have)


def from_root(value, axis, size):
    index = lax.axis_index(axis)
    dist = size // 2
    while dist >= 1:
        got = lax.ppermute(
            value, axis, [(i, i + dist) for i in range(size) if i % (2 * dist) == 0]
        )
        value = jnp.where(index % (2 * dist) == dist, got, value)
        dist //= 2
    return value


def make_local(rows_size, cols_size):
    def local(matrix):
        block_count, width, local_rows = matrix.shape
        current = matrix.reshape(block_count * width, local_rows)
        global_rows = lax.axis_index("rows") * local_rows + jnp.arange(local_rows, dtype=jnp.int32)
        identity = jnp.eye(width, dtype=jnp.float32)
        lanes = jnp.arange(width, dtype=jnp.int32)[:, None]
        units = [
            (lanes == (global_rows - k * width)[None, :]).astype(jnp.float32) for k in range(2)
        ]

        if butterfly_steps(cols_size) is None:
            gathered = lax.all_gather(current, "cols")
            panel_0 = gathered[0]
            second = gathered[1]
            head = butterfly_sum(
                inner_rows(panel_0, jnp.concatenate([panel_0, units[0]])), "rows", rows_size
            )
        else:
            head = inner_rows(current, jnp.concatenate([current, units[0]]))
            head = butterfly_sum(from_root(head, "cols", cols_size), "rows", rows_size)
            panel_0, second = spread_pair(current, "cols", cols_size)

        both = jnp.concatenate([current, second])
        tail = jnp.concatenate([inner_rows(panel_0, both), inner_rows(units[0], both)], axis=1)
        steps = butterfly_steps(rows_size)
        tail = butterfly_sum(tail, "rows", rows_size, None if steps is None else steps[:-1])
        lower_inv, tail = lax.optimization_barrier((lower_inverse(head), tail))
        tail = butterfly_sum(tail, "rows", rows_size, None if steps is None else steps[-1:])
        top_rows = head[:, width:]
        basis_cur, basis_sec, unit_cur, unit_sec = (
            tail[:, i * width:(i + 1) * width] for i in range(4)
        )
        top_block = apply_left(lower_inv, top_rows)
        inverse = invert_near_identity(identity - top_block.T)
        reflect = units[0] - apply_left(lower_inv, panel_0)
        mixed = apply_left(inverse, unit_cur - apply_left(lower_inv, basis_cur))
        mixed_sec = apply_left(inverse, unit_sec - apply_left(lower_inv, basis_sec))
        current = current - jnp.dot(mixed.T, reflect, precision=HIGHEST_PRECISION)
        second = second - jnp.dot(mixed_sec.T, reflect, precision=HIGHEST_PRECISION)

        panel_1 = jnp.where((global_rows >= width)[None, :], second, jnp.zeros_like(second))
        head = butterfly_sum(
            inner_rows(panel_1, jnp.concatenate([panel_1, units[1]])), "rows", rows_size
        )
        tail = butterfly_sum(
            jnp.concatenate([inner_rows(panel_1, current), inner_rows(units[1], current)], axis=1),
            "rows",
            rows_size,
        )
        top_rows = head[:, width:]
        basis_cur, unit_cur = tail[:, :width], tail[:, width:]
        lower_inv = lower_inverse(head)
        top_block = apply_left(lower_inv, top_rows)
        inverse = invert_near_identity(identity - top_block.T)
        reflect = units[1] - apply_left(lower_inv, panel_1)
        mixed = apply_left(inverse, unit_cur - apply_left(lower_inv, basis_cur))
        current = current - jnp.dot(mixed.T, reflect, precision=HIGHEST_PRECISION)
        return current.reshape(matrix.shape)

    return local


def solution(mesh):
    return jax.shard_map(
        make_local(mesh.shape["rows"], mesh.shape["cols"]),
        mesh=mesh,
        in_specs=(P(None, "cols", "rows"),),
        out_specs=P(None, "cols", "rows"),
        check_vma=False,
    )
```

```python
import jax
import jax.numpy as jnp
from jax import lax
from jax.experimental import pallas as pl
from jax.sharding import PartitionSpec as P

HIGHEST_PRECISION = lax.Precision.HIGHEST


def inner_rows(left, right):
    return lax.dot_general(left, right, (((1,), (1,)), ((), ())), precision=HIGHEST_PRECISION)


def apply_left(square, right_side):
    return jnp.dot(square, right_side, precision=HIGHEST_PRECISION)


def butterfly_steps(size):
    if size < 2 or size & (size - 1):
        return None
    return [1 << k for k in range(size.bit_length() - 1)]


def butterfly_sum(x, axis, size, steps=None):
    every = butterfly_steps(size)
    if every is None:
        return x if steps == [] else lax.psum(x, axis)
    for step in every if steps is None else steps:
        x = x + lax.ppermute(x, axis, [(i, i ^ step) for i in range(size)])
    return x


def invert_near_identity(square):
    identity = jnp.eye(square.shape[0], dtype=jnp.float32)
    approx = square.T * (2.0 / 4.25)
    for _ in range(7):
        approx = apply_left(approx, 2.0 * identity - apply_left(square, approx))
    return approx


def _eliminate_kernel(head_ref, out_ref):
    size = out_ref.shape[0]
    wide = 2 * size
    rows = lax.broadcasted_iota(jnp.int32, (size, wide), 0)
    lanes = lax.broadcasted_iota(jnp.int32, (size, wide), 1)
    row_ids = lax.broadcasted_iota(jnp.int32, (size, 1), 0)
    work = head_ref[:, :wide]
    work = jnp.where(lanes < size, work, (lanes == rows + size).astype(jnp.float32))
    for j in range(size):
        row = work[j:j + 1, :]
        pivot = row[:, j:j + 1]
        scale = lax.rsqrt(pivot)
        scale = scale * (1.5 - 0.5 * pivot * scale * scale)
        scaled = row * scale
        weight = jnp.where(row_ids > j, work[:, j:j + 1] * scale, 0.0)
        work = jnp.where(rows == j, scaled, work - weight * scaled)
    out_ref[...] = work[:, size:]


def lower_inverse(head):
    size = head.shape[0]
    return pl.pallas_call(
        _eliminate_kernel, out_shape=jax.ShapeDtypeStruct((size, size), jnp.float32)
    )(head)


def spread_pair(block, axis, size):
    index = lax.axis_index(axis)
    have = block
    dist = size // 2
    while dist >= 2:
        got = lax.ppermute(
            have, axis, [(i, i + dist) for i in range(size) if i % (2 * dist) < 2]
        )
        have = jnp.where(index % (2 * dist) >= dist, got, have)
        dist //= 2
    other = lax.ppermute(have, axis, [(i, i ^ 1) for i in range(size)])
    even = index % 2 == 0
    return jnp.where(even, have, other), jnp.where(even, other, have)


def from_root(value, axis, size):
    index = lax.axis_index(axis)
    dist = size // 2
    while dist >= 1:
        got = lax.ppermute(
            value, axis, [(i, i + dist) for i in range(size) if i % (2 * dist) == 0]
        )
        value = jnp.where(index % (2 * dist) == dist, got, value)
        dist //= 2
    return value


def make_local(rows_size, cols_size):
    def local(matrix):
        block_count, width, local_rows = matrix.shape
        current = matrix.reshape(block_count * width, local_rows)
        global_rows = lax.axis_index("rows") * local_rows + jnp.arange(local_rows, dtype=jnp.int32)
        identity = jnp.eye(width, dtype=jnp.float32)
        lanes = jnp.arange(width, dtype=jnp.int32)[:, None]
        units = [
            (lanes == (global_rows - k * width)[None, :]).astype(jnp.float32) for k in range(2)
        ]

        if butterfly_steps(cols_size) is None:
            gathered = lax.all_gather(current, "cols")
            panel_0 = gathered[0]
            second = gathered[1]
            head = butterfly_sum(
                inner_rows(panel_0, jnp.concatenate([panel_0, units[0]])), "rows", rows_size
            )
        else:
            head = inner_rows(current, jnp.concatenate([current, units[0]]))
            head = butterfly_sum(from_root(head, "cols", cols_size), "rows", rows_size)
            panel_0, second = spread_pair(current, "cols", cols_size)

        both = jnp.concatenate([current, second])
        tail = jnp.concatenate([inner_rows(panel_0, both), inner_rows(units[0], both)], axis=1)
        steps = butterfly_steps(rows_size)
        tail = butterfly_sum(tail, "rows", rows_size, None if steps is None else steps[:-1])
        lower_inv, tail = lax.optimization_barrier((lower_inverse(head), tail))
        tail = butterfly_sum(tail, "rows", rows_size, None if steps is None else steps[-1:])
        top_rows = head[:, width:]
        basis_cur, basis_sec, unit_cur, unit_sec = (
            tail[:, i * width:(i + 1) * width] for i in range(4)
        )
        top_block = apply_left(lower_inv, top_rows)
        inverse = invert_near_identity(identity - top_block.T)
        reflect = units[0] - apply_left(lower_inv, panel_0)
        mixed = apply_left(inverse, unit_cur - apply_left(lower_inv, basis_cur))
        mixed_sec = apply_left(inverse, unit_sec - apply_left(lower_inv, basis_sec))
        current = current - jnp.dot(mixed.T, reflect, precision=HIGHEST_PRECISION)
        second = second - jnp.dot(mixed_sec.T, reflect, precision=HIGHEST_PRECISION)

        panel_1 = jnp.where((global_rows >= width)[None, :], second, jnp.zeros_like(second))
        sums = butterfly_sum(
            jnp.concatenate(
                [inner_rows(panel_1, jnp.concatenate([panel_1, units[1]])),
                 inner_rows(panel_1, current), inner_rows(units[1], current)],
                axis=1,
            ),
            "rows",
            rows_size,
        )
        top_rows = sums[:, width:2 * width]
        basis_cur, unit_cur = sums[:, 2 * width:3 * width], sums[:, 3 * width:]
        lower_inv = lower_inverse(sums)
        top_block = apply_left(lower_inv, top_rows)
        inverse = invert_near_identity(identity - top_block.T)
        reflect = units[1] - apply_left(lower_inv, panel_1)
        mixed = apply_left(inverse, unit_cur - apply_left(lower_inv, basis_cur))
        current = current - jnp.dot(mixed.T, reflect, precision=HIGHEST_PRECISION)
        return current.reshape(matrix.shape)

    return local


def solution(mesh):
    return jax.shard_map(
        make_local(mesh.shape["rows"], mesh.shape["cols"]),
        mesh=mesh,
        in_specs=(P(None, "cols", "rows"),),
        out_specs=P(None, "cols", "rows"),
        check_vma=False,
    )
```

```python
import jax
import jax.numpy as jnp
from jax import lax
from jax.experimental import pallas as pl
from jax.sharding import PartitionSpec as P

HIGHEST_PRECISION = lax.Precision.HIGHEST


def inner_rows(left, right):
    return lax.dot_general(left, right, (((1,), (1,)), ((), ())), precision=HIGHEST_PRECISION)


def apply_left(square, right_side):
    return jnp.dot(square, right_side, precision=HIGHEST_PRECISION)


def reflect_update(block, mixed, lower_inv, unit_rows, panel):
    weights = jnp.concatenate([mixed, -jnp.dot(lower_inv.T, mixed, precision=HIGHEST_PRECISION)])
    return block - lax.dot_general(
        weights, jnp.concatenate([unit_rows, panel]), (((0,), (0,)), ((), ())),
        precision=HIGHEST_PRECISION,
    )


def butterfly_steps(size):
    if size < 2 or size & (size - 1):
        return None
    return [1 << k for k in range(size.bit_length() - 1)]


def butterfly_sum(x, axis, size, steps=None):
    every = butterfly_steps(size)
    if every is None:
        return x if steps == [] else lax.psum(x, axis)
    for step in every if steps is None else steps:
        x = x + lax.ppermute(x, axis, [(i, i ^ step) for i in range(size)])
    return x


def invert_near_identity(square):
    identity = jnp.eye(square.shape[0], dtype=jnp.float32)
    approx = square.T * (2.0 / 4.25)
    for _ in range(7):
        approx = apply_left(approx, 2.0 * identity - apply_left(square, approx))
    return approx


def _eliminate_kernel(head_ref, out_ref):
    size = out_ref.shape[0]
    wide = 2 * size
    rows = lax.broadcasted_iota(jnp.int32, (size, wide), 0)
    lanes = lax.broadcasted_iota(jnp.int32, (size, wide), 1)
    row_ids = lax.broadcasted_iota(jnp.int32, (size, 1), 0)
    work = head_ref[:, :wide]
    work = jnp.where(lanes < size, work, (lanes == rows + size).astype(jnp.float32))
    for j in range(size):
        row = work[j:j + 1, :]
        pivot = row[:, j:j + 1]
        scale = lax.rsqrt(pivot)
        scale = scale * (1.5 - 0.5 * pivot * scale * scale)
        scaled = row * scale
        weight = jnp.where(row_ids > j, work[:, j:j + 1] * scale, 0.0)
        work = jnp.where(rows == j, scaled, work - weight * scaled)
    out_ref[...] = work[:, size:]


def lower_inverse(head):
    size = head.shape[0]
    return pl.pallas_call(
        _eliminate_kernel, out_shape=jax.ShapeDtypeStruct((size, size), jnp.float32)
    )(head)


def spread_pair(block, axis, size):
    index = lax.axis_index(axis)
    have = block
    dist = size // 2
    while dist >= 2:
        got = lax.ppermute(
            have, axis, [(i, i + dist) for i in range(size) if i % (2 * dist) < 2]
        )
        have = jnp.where(index % (2 * dist) >= dist, got, have)
        dist //= 2
    other = lax.ppermute(have, axis, [(i, i ^ 1) for i in range(size)])
    even = index % 2 == 0
    return jnp.where(even, have, other), jnp.where(even, other, have)


def from_root(value, axis, size):
    index = lax.axis_index(axis)
    dist = size // 2
    while dist >= 1:
        got = lax.ppermute(
            value, axis, [(i, i + dist) for i in range(size) if i % (2 * dist) == 0]
        )
        value = jnp.where(index % (2 * dist) == dist, got, value)
        dist //= 2
    return value


def make_local(rows_size, cols_size):
    def local(matrix):
        block_count, width, local_rows = matrix.shape
        current = matrix.reshape(block_count * width, local_rows)
        global_rows = lax.axis_index("rows") * local_rows + jnp.arange(local_rows, dtype=jnp.int32)
        identity = jnp.eye(width, dtype=jnp.float32)
        lanes = jnp.arange(width, dtype=jnp.int32)[:, None]
        units = [
            (lanes == (global_rows - k * width)[None, :]).astype(jnp.float32) for k in range(2)
        ]

        if butterfly_steps(cols_size) is None:
            gathered = lax.all_gather(current, "cols")
            panel_0 = gathered[0]
            second = gathered[1]
            head = butterfly_sum(
                inner_rows(panel_0, jnp.concatenate([panel_0, units[0]])), "rows", rows_size
            )
        else:
            head = inner_rows(current, jnp.concatenate([current, units[0]]))
            head = butterfly_sum(from_root(head, "cols", cols_size), "rows", rows_size)
            panel_0, second = spread_pair(current, "cols", cols_size)

        both = jnp.concatenate([current, second])
        tail = jnp.concatenate([inner_rows(panel_0, both), inner_rows(units[0], both)], axis=1)
        steps = butterfly_steps(rows_size)
        tail = butterfly_sum(tail, "rows", rows_size, None if steps is None else steps[:-1])
        lower_inv, tail = lax.optimization_barrier((lower_inverse(head), tail))
        tail = butterfly_sum(tail, "rows", rows_size, None if steps is None else steps[-1:])
        top_rows = head[:, width:]
        basis_cur, basis_sec, unit_cur, unit_sec = (
            tail[:, i * width:(i + 1) * width] for i in range(4)
        )
        top_block = apply_left(lower_inv, top_rows)
        inverse = invert_near_identity(identity - top_block.T)
        mixed = apply_left(inverse, unit_cur - apply_left(lower_inv, basis_cur))
        mixed_sec = apply_left(inverse, unit_sec - apply_left(lower_inv, basis_sec))
        current = reflect_update(current, mixed, lower_inv, units[0], panel_0)
        second = reflect_update(second, mixed_sec, lower_inv, units[0], panel_0)

        panel_1 = jnp.where((global_rows >= width)[None, :], second, jnp.zeros_like(second))
        head = butterfly_sum(
            inner_rows(panel_1, jnp.concatenate([panel_1, units[1]])), "rows", rows_size
        )
        tail = butterfly_sum(
            jnp.concatenate([inner_rows(panel_1, current), inner_rows(units[1], current)], axis=1),
            "rows",
            rows_size,
        )
        top_rows = head[:, width:]
        basis_cur, unit_cur = tail[:, :width], tail[:, width:]
        lower_inv = lower_inverse(head)
        top_block = apply_left(lower_inv, top_rows)
        inverse = invert_near_identity(identity - top_block.T)
        mixed = apply_left(inverse, unit_cur - apply_left(lower_inv, basis_cur))
        current = reflect_update(current, mixed, lower_inv, units[1], panel_1)
        return current.reshape(matrix.shape)

    return local


def solution(mesh):
    return jax.shard_map(
        make_local(mesh.shape["rows"], mesh.shape["cols"]),
        mesh=mesh,
        in_specs=(P(None, "cols", "rows"),),
        out_specs=P(None, "cols", "rows"),
        check_vma=False,
    )
```

```python
import jax
import jax.numpy as jnp
from jax import lax
from jax.experimental import pallas as pl
from jax.sharding import PartitionSpec as P

HIGHEST_PRECISION = lax.Precision.HIGHEST


def inner_rows(left, right):
    return lax.dot_general(left, right, (((1,), (1,)), ((), ())), precision=HIGHEST_PRECISION)


def apply_left(square, right_side):
    return jnp.dot(square, right_side, precision=HIGHEST_PRECISION)


def butterfly_steps(size):
    if size < 2 or size & (size - 1):
        return None
    return [1 << k for k in range(size.bit_length() - 1)]


def butterfly_sum(x, axis, size, steps=None):
    every = butterfly_steps(size)
    if every is None:
        return x if steps == [] else lax.psum(x, axis)
    for step in every if steps is None else steps:
        x = x + lax.ppermute(x, axis, [(i, i ^ step) for i in range(size)])
    return x


def invert_near_identity(square):
    identity = jnp.eye(square.shape[0], dtype=jnp.float32)
    approx = square.T * (2.0 / 4.25)
    for _ in range(7):
        approx = apply_left(approx, 2.0 * identity - apply_left(square, approx))
    return approx


def _eliminate_kernel(head_ref, out_ref):
    size = out_ref.shape[0]
    wide = 2 * size
    rows = lax.broadcasted_iota(jnp.int32, (size, wide), 0)
    lanes = lax.broadcasted_iota(jnp.int32, (size, wide), 1)
    row_ids = lax.broadcasted_iota(jnp.int32, (size, 1), 0)
    work = head_ref[:, :wide]
    work = jnp.where(lanes < size, work, (lanes == rows + size).astype(jnp.float32))
    for j in range(size):
        row = work[j:j + 1, :]
        pivot = row[:, j:j + 1]
        scale = lax.rsqrt(pivot)
        scaled = row * scale
        weight = jnp.where(row_ids > j, work[:, j:j + 1] * scale, 0.0)
        work = jnp.where(rows == j, scaled, work - weight * scaled)
    out_ref[...] = work[:, size:]


def lower_inverse(head):
    size = head.shape[0]
    return pl.pallas_call(
        _eliminate_kernel, out_shape=jax.ShapeDtypeStruct((size, size), jnp.float32)
    )(head)


def spread_pair(block, axis, size):
    index = lax.axis_index(axis)
    have = block
    dist = size // 2
    while dist >= 2:
        got = lax.ppermute(
            have, axis, [(i, i + dist) for i in range(size) if i % (2 * dist) < 2]
        )
        have = jnp.where(index % (2 * dist) >= dist, got, have)
        dist //= 2
    other = lax.ppermute(have, axis, [(i, i ^ 1) for i in range(size)])
    even = index % 2 == 0
    return jnp.where(even, have, other), jnp.where(even, other, have)


def from_root(value, axis, size):
    index = lax.axis_index(axis)
    dist = size // 2
    while dist >= 1:
        got = lax.ppermute(
            value, axis, [(i, i + dist) for i in range(size) if i % (2 * dist) == 0]
        )
        value = jnp.where(index % (2 * dist) == dist, got, value)
        dist //= 2
    return value


def make_local(rows_size, cols_size):
    def local(matrix):
        block_count, width, local_rows = matrix.shape
        current = matrix.reshape(block_count * width, local_rows)
        global_rows = lax.axis_index("rows") * local_rows + jnp.arange(local_rows, dtype=jnp.int32)
        identity = jnp.eye(width, dtype=jnp.float32)
        lanes = jnp.arange(width, dtype=jnp.int32)[:, None]
        units = [
            (lanes == (global_rows - k * width)[None, :]).astype(jnp.float32) for k in range(2)
        ]

        if butterfly_steps(cols_size) is None:
            gathered = lax.all_gather(current, "cols")
            panel_0 = gathered[0]
            second = gathered[1]
            head = butterfly_sum(
                inner_rows(panel_0, jnp.concatenate([panel_0, units[0]])), "rows", rows_size
            )
        else:
            head = inner_rows(current, jnp.concatenate([current, units[0]]))
            head = butterfly_sum(from_root(head, "cols", cols_size), "rows", rows_size)
            panel_0, second = spread_pair(current, "cols", cols_size)

        both = jnp.concatenate([current, second])
        tail = jnp.concatenate([inner_rows(panel_0, both), inner_rows(units[0], both)], axis=1)
        steps = butterfly_steps(rows_size)
        tail = butterfly_sum(tail, "rows", rows_size, None if steps is None else steps[:-1])
        head, tail = lax.optimization_barrier((head, tail))
        tail = butterfly_sum(tail, "rows", rows_size, None if steps is None else steps[-1:])
        lower_inv = lower_inverse(head)
        top_rows = head[:, width:]
        basis_cur, basis_sec, unit_cur, unit_sec = (
            tail[:, i * width:(i + 1) * width] for i in range(4)
        )
        top_block = apply_left(lower_inv, top_rows)
        inverse = invert_near_identity(identity - top_block.T)
        reflect = units[0] - apply_left(lower_inv, panel_0)
        mixed = apply_left(inverse, unit_cur - apply_left(lower_inv, basis_cur))
        mixed_sec = apply_left(inverse, unit_sec - apply_left(lower_inv, basis_sec))
        current = current - jnp.dot(mixed.T, reflect, precision=HIGHEST_PRECISION)
        second = second - jnp.dot(mixed_sec.T, reflect, precision=HIGHEST_PRECISION)

        panel_1 = jnp.where((global_rows >= width)[None, :], second, jnp.zeros_like(second))
        head = butterfly_sum(
            inner_rows(panel_1, jnp.concatenate([panel_1, units[1]])), "rows", rows_size
        )
        tail = butterfly_sum(
            jnp.concatenate([inner_rows(panel_1, current), inner_rows(units[1], current)], axis=1),
            "rows",
            rows_size,
        )
        top_rows = head[:, width:]
        basis_cur, unit_cur = tail[:, :width], tail[:, width:]
        lower_inv = lower_inverse(head)
        top_block = apply_left(lower_inv, top_rows)
        inverse = invert_near_identity(identity - top_block.T)
        reflect = units[1] - apply_left(lower_inv, panel_1)
        mixed = apply_left(inverse, unit_cur - apply_left(lower_inv, basis_cur))
        current = current - jnp.dot(mixed.T, reflect, precision=HIGHEST_PRECISION)
        return current.reshape(matrix.shape)

    return local


def solution(mesh):
    return jax.shard_map(
        make_local(mesh.shape["rows"], mesh.shape["cols"]),
        mesh=mesh,
        in_specs=(P(None, "cols", "rows"),),
        out_specs=P(None, "cols", "rows"),
        check_vma=False,
    )
```

```python
import jax
import jax.numpy as jnp
from jax import lax
from jax.experimental import pallas as pl
from jax.sharding import PartitionSpec as P

HIGHEST_PRECISION = lax.Precision.HIGHEST


def inner_rows(left, right):
    return lax.dot_general(left, right, (((1,), (1,)), ((), ())), precision=HIGHEST_PRECISION)


def apply_left(square, right_side):
    return jnp.dot(square, right_side, precision=HIGHEST_PRECISION)


def butterfly_steps(size):
    if size < 2 or size & (size - 1):
        return None
    return [1 << k for k in range(size.bit_length() - 1)]


def butterfly_sum(x, axis, size, steps=None):
    every = butterfly_steps(size)
    if every is None:
        return x if steps == [] else lax.psum(x, axis)
    for step in every if steps is None else steps:
        x = x + lax.ppermute(x, axis, [(i, i ^ step) for i in range(size)])
    return x


def invert_near_identity(square):
    identity = jnp.eye(square.shape[0], dtype=jnp.float32)
    approx = square.T * (2.0 / 4.25)
    for _ in range(7):
        approx = apply_left(approx, 2.0 * identity - apply_left(square, approx))
    return approx


def _eliminate_kernel(head_ref, out_ref):
    size = out_ref.shape[0]
    wide = 2 * size
    rows = lax.broadcasted_iota(jnp.int32, (size, wide), 0)
    lanes = lax.broadcasted_iota(jnp.int32, (size, wide), 1)
    row_ids = lax.broadcasted_iota(jnp.int32, (size, 1), 0)
    work = head_ref[:, :wide]
    work = jnp.where(lanes < size, work, (lanes == rows + size).astype(jnp.float32))
    for j in range(size):
        row = work[j:j + 1, :]
        pivot = row[:, j:j + 1]
        scale = lax.rsqrt(pivot)
        scale = scale * (1.5 - 0.5 * pivot * scale * scale)
        scaled = row * scale
        weight = jnp.where(row_ids > j, work[:, j:j + 1] * scale, 0.0)
        work = jnp.where(rows == j, scaled, work - weight * scaled)
    out_ref[...] = work[:, size:]


def lower_inverse(head):
    size = head.shape[0]
    return pl.pallas_call(
        _eliminate_kernel, out_shape=jax.ShapeDtypeStruct((size, size), jnp.float32)
    )(head)


def spread_pair(block, value, axis, size):
    index = lax.axis_index(axis)
    length = block.shape[1]
    have = block
    dist = size // 2
    while dist >= 2:
        got = lax.ppermute(
            jnp.concatenate([have, value], axis=1),
            axis,
            [(i, i + dist) for i in range(size) if i % (2 * dist) < 2],
        )
        have = jnp.where(index % (2 * dist) >= dist, got[:, :length], have)
        value = jnp.where(index % (2 * dist) == dist, got[:, length:], value)
        dist //= 2
    got = lax.ppermute(
        jnp.concatenate([have, value], axis=1), axis, [(i, i ^ 1) for i in range(size)]
    )
    even = index % 2 == 0
    other = got[:, :length]
    value = jnp.where(even, value, got[:, length:])
    return jnp.where(even, have, other), jnp.where(even, other, have), value


def make_local(rows_size, cols_size):
    def local(matrix):
        block_count, width, local_rows = matrix.shape
        current = matrix.reshape(block_count * width, local_rows)
        global_rows = lax.axis_index("rows") * local_rows + jnp.arange(local_rows, dtype=jnp.int32)
        identity = jnp.eye(width, dtype=jnp.float32)
        lanes = jnp.arange(width, dtype=jnp.int32)[:, None]
        units = [
            (lanes == (global_rows - k * width)[None, :]).astype(jnp.float32) for k in range(2)
        ]

        if butterfly_steps(cols_size) is None:
            gathered = lax.all_gather(current, "cols")
            panel_0 = gathered[0]
            second = gathered[1]
            head = butterfly_sum(
                inner_rows(panel_0, jnp.concatenate([panel_0, units[0]])), "rows", rows_size
            )
        else:
            head = inner_rows(current, jnp.concatenate([current, units[0]]))
            panel_0, second, head = spread_pair(current, head, "cols", cols_size)
            head = butterfly_sum(head, "rows", rows_size)

        both = jnp.concatenate([current, second])
        tail = jnp.concatenate([inner_rows(panel_0, both), inner_rows(units[0], both)], axis=1)
        steps = butterfly_steps(rows_size)
        tail = butterfly_sum(tail, "rows", rows_size, None if steps is None else steps[:-1])
        lower_inv, tail = lax.optimization_barrier((lower_inverse(head), tail))
        tail = butterfly_sum(tail, "rows", rows_size, None if steps is None else steps[-1:])
        top_rows = head[:, width:]
        basis_cur, basis_sec, unit_cur, unit_sec = (
            tail[:, i * width:(i + 1) * width] for i in range(4)
        )
        top_block = apply_left(lower_inv, top_rows)
        inverse = invert_near_identity(identity - top_block.T)
        reflect = units[0] - apply_left(lower_inv, panel_0)
        mixed = apply_left(inverse, unit_cur - apply_left(lower_inv, basis_cur))
        mixed_sec = apply_left(inverse, unit_sec - apply_left(lower_inv, basis_sec))
        current = current - jnp.dot(mixed.T, reflect, precision=HIGHEST_PRECISION)
        second = second - jnp.dot(mixed_sec.T, reflect, precision=HIGHEST_PRECISION)

        panel_1 = jnp.where((global_rows >= width)[None, :], second, jnp.zeros_like(second))
        head = butterfly_sum(
            inner_rows(panel_1, jnp.concatenate([panel_1, units[1]])), "rows", rows_size
        )
        tail = butterfly_sum(
            jnp.concatenate([inner_rows(panel_1, current), inner_rows(units[1], current)], axis=1),
            "rows",
            rows_size,
        )
        top_rows = head[:, width:]
        basis_cur, unit_cur = tail[:, :width], tail[:, width:]
        lower_inv = lower_inverse(head)
        top_block = apply_left(lower_inv, top_rows)
        inverse = invert_near_identity(identity - top_block.T)
        reflect = units[1] - apply_left(lower_inv, panel_1)
        mixed = apply_left(inverse, unit_cur - apply_left(lower_inv, basis_cur))
        current = current - jnp.dot(mixed.T, reflect, precision=HIGHEST_PRECISION)
        return current.reshape(matrix.shape)

    return local


def solution(mesh):
    return jax.shard_map(
        make_local(mesh.shape["rows"], mesh.shape["cols"]),
        mesh=mesh,
        in_specs=(P(None, "cols", "rows"),),
        out_specs=P(None, "cols", "rows"),
        check_vma=False,
    )
```

```python
import jax
import jax.numpy as jnp
from jax import lax
from jax.experimental import pallas as pl
from jax.sharding import PartitionSpec as P

HIGHEST_PRECISION = lax.Precision.HIGHEST


def inner_rows(left, right):
    return lax.dot_general(left, right, (((1,), (1,)), ((), ())), precision=HIGHEST_PRECISION)


def apply_left(square, right_side):
    return jnp.dot(square, right_side, precision=HIGHEST_PRECISION)


def butterfly_steps(size):
    if size < 2 or size & (size - 1):
        return None
    return [1 << k for k in range(size.bit_length() - 1)]


def butterfly_sum(x, axis, size, steps=None):
    every = butterfly_steps(size)
    if every is None:
        return x if steps == [] else lax.psum(x, axis)
    for step in every if steps is None else steps:
        x = x + lax.ppermute(x, axis, [(i, i ^ step) for i in range(size)])
    return x


def butterfly_parts(x, axis, size):
    steps = butterfly_steps(size)
    if steps is None:
        return lax.psum(x, axis), jnp.zeros_like(x)
    x = butterfly_sum(x, axis, size, steps[:-1])
    return x, lax.ppermute(x, axis, [(i, i ^ steps[-1]) for i in range(size)])


def invert_near_identity(square):
    identity = jnp.eye(square.shape[0], dtype=jnp.float32)
    approx = square.T * (2.0 / 4.25)
    for _ in range(7):
        approx = apply_left(approx, 2.0 * identity - apply_left(square, approx))
    return approx


def _eliminate_kernel(part_ref, last_ref, out_ref):
    size = out_ref.shape[0]
    wide = 2 * size
    rows = lax.broadcasted_iota(jnp.int32, (size, wide), 0)
    lanes = lax.broadcasted_iota(jnp.int32, (size, wide), 1)
    row_ids = lax.broadcasted_iota(jnp.int32, (size, 1), 0)
    work = part_ref[:, :wide] + last_ref[:, :wide]
    work = jnp.where(lanes < size, work, (lanes == rows + size).astype(jnp.float32))
    for j in range(size):
        row = work[j:j + 1, :]
        pivot = row[:, j:j + 1]
        scale = lax.rsqrt(pivot)
        scaled = row * scale
        weight = jnp.where(row_ids > j, work[:, j:j + 1] * scale, 0.0)
        work = jnp.where(rows == j, scaled, work - weight * scaled)
    out_ref[...] = work[:, size:]


def lower_inverse(parts):
    size = parts[0].shape[0]
    return pl.pallas_call(
        _eliminate_kernel, out_shape=jax.ShapeDtypeStruct((size, size), jnp.float32)
    )(*parts)


def spread_pair(block, axis, size):
    index = lax.axis_index(axis)
    have = block
    dist = size // 2
    while dist >= 2:
        got = lax.ppermute(
            have, axis, [(i, i + dist) for i in range(size) if i % (2 * dist) < 2]
        )
        have = jnp.where(index % (2 * dist) >= dist, got, have)
        dist //= 2
    other = lax.ppermute(have, axis, [(i, i ^ 1) for i in range(size)])
    even = index % 2 == 0
    return jnp.where(even, have, other), jnp.where(even, other, have)


def from_root(value, axis, size):
    index = lax.axis_index(axis)
    dist = size // 2
    while dist >= 1:
        got = lax.ppermute(
            value, axis, [(i, i + dist) for i in range(size) if i % (2 * dist) == 0]
        )
        value = jnp.where(index % (2 * dist) == dist, got, value)
        dist //= 2
    return value


def make_local(rows_size, cols_size):
    def local(matrix):
        block_count, width, local_rows = matrix.shape
        current = matrix.reshape(block_count * width, local_rows)
        global_rows = lax.axis_index("rows") * local_rows + jnp.arange(local_rows, dtype=jnp.int32)
        identity = jnp.eye(width, dtype=jnp.float32)
        lanes = jnp.arange(width, dtype=jnp.int32)[:, None]
        units = [
            (lanes == (global_rows - k * width)[None, :]).astype(jnp.float32) for k in range(2)
        ]

        if butterfly_steps(cols_size) is None:
            gathered = lax.all_gather(current, "cols")
            panel_0 = gathered[0]
            second = gathered[1]
            head = butterfly_parts(
                inner_rows(panel_0, jnp.concatenate([panel_0, units[0]])), "rows", rows_size
            )
        else:
            head = inner_rows(current, jnp.concatenate([current, units[0]]))
            head = butterfly_parts(from_root(head, "cols", cols_size), "rows", rows_size)
            panel_0, second = spread_pair(current, "cols", cols_size)

        both = jnp.concatenate([current, second])
        tail = jnp.concatenate([inner_rows(panel_0, both), inner_rows(units[0], both)], axis=1)
        steps = butterfly_steps(rows_size)
        tail = butterfly_sum(tail, "rows", rows_size, None if steps is None else steps[:-1])
        lower_inv, tail = lax.optimization_barrier((lower_inverse(head), tail))
        tail = butterfly_sum(tail, "rows", rows_size, None if steps is None else steps[-1:])
        top_rows = (head[0] + head[1])[:, width:]
        basis_cur, basis_sec, unit_cur, unit_sec = (
            tail[:, i * width:(i + 1) * width] for i in range(4)
        )
        top_block = apply_left(lower_inv, top_rows)
        inverse = invert_near_identity(identity - top_block.T)
        reflect = units[0] - apply_left(lower_inv, panel_0)
        mixed = apply_left(inverse, unit_cur - apply_left(lower_inv, basis_cur))
        mixed_sec = apply_left(inverse, unit_sec - apply_left(lower_inv, basis_sec))
        current = current - jnp.dot(mixed.T, reflect, precision=HIGHEST_PRECISION)
        second = second - jnp.dot(mixed_sec.T, reflect, precision=HIGHEST_PRECISION)

        panel_1 = jnp.where((global_rows >= width)[None, :], second, jnp.zeros_like(second))
        head = butterfly_parts(
            inner_rows(panel_1, jnp.concatenate([panel_1, units[1]])), "rows", rows_size
        )
        tail = butterfly_sum(
            jnp.concatenate([inner_rows(panel_1, current), inner_rows(units[1], current)], axis=1),
            "rows",
            rows_size,
        )
        top_rows = (head[0] + head[1])[:, width:]
        basis_cur, unit_cur = tail[:, :width], tail[:, width:]
        lower_inv = lower_inverse(head)
        top_block = apply_left(lower_inv, top_rows)
        inverse = invert_near_identity(identity - top_block.T)
        reflect = units[1] - apply_left(lower_inv, panel_1)
        mixed = apply_left(inverse, unit_cur - apply_left(lower_inv, basis_cur))
        current = current - jnp.dot(mixed.T, reflect, precision=HIGHEST_PRECISION)
        return current.reshape(matrix.shape)

    return local


def solution(mesh):
    return jax.shard_map(
        make_local(mesh.shape["rows"], mesh.shape["cols"]),
        mesh=mesh,
        in_specs=(P(None, "cols", "rows"),),
        out_specs=P(None, "cols", "rows"),
        check_vma=False,
    )
```

```python
import jax
import jax.numpy as jnp
from jax import lax
from jax.experimental import pallas as pl
from jax.sharding import PartitionSpec as P

HIGHEST_PRECISION = lax.Precision.HIGHEST


def inner_rows(left, right):
    return lax.dot_general(left, right, (((1,), (1,)), ((), ())), precision=HIGHEST_PRECISION)


def apply_left(square, right_side):
    return jnp.dot(square, right_side, precision=HIGHEST_PRECISION)


def butterfly_steps(size):
    if size < 2 or size & (size - 1):
        return None
    return [1 << k for k in range(size.bit_length() - 1)]


def butterfly_sum(x, axis, size, steps=None):
    every = butterfly_steps(size)
    if every is None:
        return x if steps == [] else lax.psum(x, axis)
    for step in every if steps is None else steps:
        x = x + lax.ppermute(x, axis, [(i, i ^ step) for i in range(size)])
    return x


def invert_near_identity(square):
    identity = jnp.eye(square.shape[0], dtype=jnp.float32)
    approx = square.T * (2.0 / (0.25 + 4.84))
    for _ in range(8):
        approx = apply_left(approx, 2.0 * identity - apply_left(square, approx))
    return approx


def _eliminate_kernel(head_ref, out_ref):
    size = out_ref.shape[0]
    wide = 2 * size
    rows = lax.broadcasted_iota(jnp.int32, (size, wide), 0)
    lanes = lax.broadcasted_iota(jnp.int32, (size, wide), 1)
    row_ids = lax.broadcasted_iota(jnp.int32, (size, 1), 0)
    work = head_ref[:, :wide]
    work = jnp.where(lanes < size, work, (lanes == rows + size).astype(jnp.float32))
    for j in range(size):
        row = work[j:j + 1, :]
        pivot = row[:, j:j + 1]
        scale = lax.rsqrt(pivot)
        scale = scale * (1.5 - 0.5 * pivot * scale * scale)
        scaled = row * scale
        weight = jnp.where(row_ids > j, work[:, j:j + 1] * scale, 0.0)
        work = jnp.where(rows == j, scaled, work - weight * scaled)
    out_ref[...] = work[:, size:]


def lower_inverse(head):
    size = head.shape[0]
    return pl.pallas_call(
        _eliminate_kernel, out_shape=jax.ShapeDtypeStruct((size, size), jnp.float32)
    )(head)


def spread_pair(block, axis, size):
    index = lax.axis_index(axis)
    have = block
    dist = size // 2
    while dist >= 2:
        got = lax.ppermute(
            have, axis, [(i, i + dist) for i in range(size) if i % (2 * dist) < 2]
        )
        have = jnp.where(index % (2 * dist) >= dist, got, have)
        dist //= 2
    other = lax.ppermute(have, axis, [(i, i ^ 1) for i in range(size)])
    even = index % 2 == 0
    return jnp.where(even, have, other), jnp.where(even, other, have)


def from_root(value, axis, size):
    index = lax.axis_index(axis)
    dist = size // 2
    while dist >= 1:
        got = lax.ppermute(
            value, axis, [(i, i + dist) for i in range(size) if i % (2 * dist) == 0]
        )
        value = jnp.where(index % (2 * dist) == dist, got, value)
        dist //= 2
    return value


def make_local(rows_size, cols_size):
    def local(matrix):
        block_count, width, local_rows = matrix.shape
        current = matrix.reshape(block_count * width, local_rows)
        global_rows = lax.axis_index("rows") * local_rows + jnp.arange(local_rows, dtype=jnp.int32)
        identity = jnp.eye(width, dtype=jnp.float32)
        lanes = jnp.arange(width, dtype=jnp.int32)[:, None]
        units = [
            (lanes == (global_rows - k * width)[None, :]).astype(jnp.float32) for k in range(2)
        ]

        if butterfly_steps(cols_size) is None:
            gathered = lax.all_gather(current, "cols")
            panel_0 = gathered[0]
            second = gathered[1]
            head = butterfly_sum(
                inner_rows(panel_0, jnp.concatenate([panel_0, units[0]])), "rows", rows_size
            )
        else:
            head = inner_rows(current, jnp.concatenate([current, units[0]]))
            head = butterfly_sum(from_root(head, "cols", cols_size), "rows", rows_size)
            panel_0, second = spread_pair(current, "cols", cols_size)

        both = jnp.concatenate([current, second])
        tail = jnp.concatenate([inner_rows(panel_0, both), inner_rows(units[0], both)], axis=1)
        steps = butterfly_steps(rows_size)
        tail = butterfly_sum(tail, "rows", rows_size, None if steps is None else steps[:-1])
        lower_inv, tail = lax.optimization_barrier((lower_inverse(head), tail))
        tail = butterfly_sum(tail, "rows", rows_size, None if steps is None else steps[-1:])
        top_rows = head[:, width:]
        basis_cur, basis_sec, unit_cur, unit_sec = (
            tail[:, i * width:(i + 1) * width] for i in range(4)
        )
        top_block = apply_left(lower_inv, top_rows)
        inverse = invert_near_identity(identity - top_block.T)
        reflect = units[0] - apply_left(lower_inv, panel_0)
        mixed = apply_left(inverse, unit_cur - apply_left(lower_inv, basis_cur))
        mixed_sec = apply_left(inverse, unit_sec - apply_left(lower_inv, basis_sec))
        current = current - jnp.dot(mixed.T, reflect, precision=HIGHEST_PRECISION)
        second = second - jnp.dot(mixed_sec.T, reflect, precision=HIGHEST_PRECISION)

        panel_1 = jnp.where((global_rows >= width)[None, :], second, jnp.zeros_like(second))
        head = butterfly_sum(
            inner_rows(panel_1, jnp.concatenate([panel_1, units[1]])), "rows", rows_size
        )
        tail = butterfly_sum(
            jnp.concatenate([inner_rows(panel_1, current), inner_rows(units[1], current)], axis=1),
            "rows",
            rows_size,
        )
        top_rows = head[:, width:]
        basis_cur, unit_cur = tail[:, :width], tail[:, width:]
        lower_inv = lower_inverse(head)
        top_block = apply_left(lower_inv, top_rows)
        inverse = invert_near_identity(identity - top_block.T)
        reflect = units[1] - apply_left(lower_inv, panel_1)
        mixed = apply_left(inverse, unit_cur - apply_left(lower_inv, basis_cur))
        current = current - jnp.dot(mixed.T, reflect, precision=HIGHEST_PRECISION)
        return current.reshape(matrix.shape)

    return local


def solution(mesh):
    return jax.shard_map(
        make_local(mesh.shape["rows"], mesh.shape["cols"]),
        mesh=mesh,
        in_specs=(P(None, "cols", "rows"),),
        out_specs=P(None, "cols", "rows"),
        check_vma=False,
    )
```

```python
import jax
import jax.numpy as jnp
from jax import lax
from jax.experimental import pallas as pl
from jax.sharding import PartitionSpec as P

HIGHEST_PRECISION = lax.Precision.HIGHEST


def inner_rows(left, right):
    return lax.dot_general(left, right, (((1,), (1,)), ((), ())), precision=HIGHEST_PRECISION)


def apply_left(square, right_side):
    return jnp.dot(square, right_side, precision=HIGHEST_PRECISION)


def butterfly_steps(size):
    if size < 2 or size & (size - 1):
        return None
    return [1 << k for k in range(size.bit_length() - 1)]


def butterfly_sum(x, axis, size, steps=None):
    every = butterfly_steps(size)
    if every is None:
        return x if steps == [] else lax.psum(x, axis)
    for step in every if steps is None else steps:
        x = x + lax.ppermute(x, axis, [(i, i ^ step) for i in range(size)])
    return x


def invert_near_identity(square):
    identity = jnp.eye(square.shape[0], dtype=jnp.float32)
    approx = square.T * (2.0 / (0.25 + 4.84))
    for _ in range(8):
        approx = apply_left(approx, 2.0 * identity - apply_left(square, approx))
    return approx


def _eliminate_kernel(head_ref, out_ref):
    size = out_ref.shape[0]
    wide = 2 * size
    rows = lax.broadcasted_iota(jnp.int32, (size, wide), 0)
    lanes = lax.broadcasted_iota(jnp.int32, (size, wide), 1)
    row_ids = lax.broadcasted_iota(jnp.int32, (size, 1), 0)
    work = head_ref[:, :wide]
    work = jnp.where(lanes < size, work, (lanes == rows + size).astype(jnp.float32))
    for j in range(size):
        row = work[j:j + 1, :]
        pivot = row[:, j:j + 1]
        scale = lax.rsqrt(pivot)
        scaled = row * scale
        weight = jnp.where(row_ids > j, work[:, j:j + 1] * scale, 0.0)
        work = jnp.where(rows == j, scaled, work - weight * scaled)
    out_ref[...] = work[:, size:]


def lower_inverse(head):
    size = head.shape[0]
    return pl.pallas_call(
        _eliminate_kernel, out_shape=jax.ShapeDtypeStruct((size, size), jnp.float32)
    )(head)


def spread_pair(block, axis, size, hold=None):
    index = lax.axis_index(axis)
    have = block
    dist = size // 2
    while dist >= 2:
        got = lax.ppermute(
            have, axis, [(i, i + dist) for i in range(size) if i % (2 * dist) < 2]
        )
        have = jnp.where(index % (2 * dist) >= dist, got, have)
        dist //= 2
    if hold is not None:
        have, hold = lax.optimization_barrier((have, hold))
    other = lax.ppermute(have, axis, [(i, i ^ 1) for i in range(size)])
    even = index % 2 == 0
    return jnp.where(even, have, other), jnp.where(even, other, have), hold


def from_root(value, axis, size):
    index = lax.axis_index(axis)
    dist = size // 2
    while dist >= 1:
        got = lax.ppermute(
            value, axis, [(i, i + dist) for i in range(size) if i % (2 * dist) == 0]
        )
        value = jnp.where(index % (2 * dist) == dist, got, value)
        dist //= 2
    return value


def make_local(rows_size, cols_size):
    def local(matrix):
        block_count, width, local_rows = matrix.shape
        current = matrix.reshape(block_count * width, local_rows)
        global_rows = lax.axis_index("rows") * local_rows + jnp.arange(local_rows, dtype=jnp.int32)
        identity = jnp.eye(width, dtype=jnp.float32)
        lanes = jnp.arange(width, dtype=jnp.int32)[:, None]
        units = [
            (lanes == (global_rows - k * width)[None, :]).astype(jnp.float32) for k in range(2)
        ]

        if butterfly_steps(cols_size) is None:
            gathered = lax.all_gather(current, "cols")
            panel_0 = gathered[0]
            second = gathered[1]
            head = butterfly_sum(
                inner_rows(panel_0, jnp.concatenate([panel_0, units[0]])), "rows", rows_size
            )
        else:
            head = inner_rows(current, jnp.concatenate([current, units[0]]))
            head = from_root(head, "cols", cols_size)
            steps = butterfly_steps(rows_size)
            head = butterfly_sum(head, "rows", rows_size, None if steps is None else steps[:1])
            panel_0, second, head = spread_pair(current, "cols", cols_size, head)
            head = butterfly_sum(head, "rows", rows_size, [] if steps is None else steps[1:])

        both = jnp.concatenate([current, second])
        tail = jnp.concatenate([inner_rows(panel_0, both), inner_rows(units[0], both)], axis=1)
        steps = butterfly_steps(rows_size)
        tail = butterfly_sum(tail, "rows", rows_size, None if steps is None else steps[:-1])
        lower_inv, tail = lax.optimization_barrier((lower_inverse(head), tail))
        tail = butterfly_sum(tail, "rows", rows_size, None if steps is None else steps[-1:])
        top_rows = head[:, width:]
        basis_cur, basis_sec, unit_cur, unit_sec = (
            tail[:, i * width:(i + 1) * width] for i in range(4)
        )
        top_block = apply_left(lower_inv, top_rows)
        inverse = invert_near_identity(identity - top_block.T)
        reflect = units[0] - apply_left(lower_inv, panel_0)
        mixed = apply_left(inverse, unit_cur - apply_left(lower_inv, basis_cur))
        mixed_sec = apply_left(inverse, unit_sec - apply_left(lower_inv, basis_sec))
        current = current - jnp.dot(mixed.T, reflect, precision=HIGHEST_PRECISION)
        second = second - jnp.dot(mixed_sec.T, reflect, precision=HIGHEST_PRECISION)

        panel_1 = jnp.where((global_rows >= width)[None, :], second, jnp.zeros_like(second))
        head = butterfly_sum(
            inner_rows(panel_1, jnp.concatenate([panel_1, units[1]])), "rows", rows_size
        )
        tail = butterfly_sum(
            jnp.concatenate([inner_rows(panel_1, current), inner_rows(units[1], current)], axis=1),
            "rows",
            rows_size,
        )
        top_rows = head[:, width:]
        basis_cur, unit_cur = tail[:, :width], tail[:, width:]
        lower_inv = lower_inverse(head)
        top_block = apply_left(lower_inv, top_rows)
        inverse = invert_near_identity(identity - top_block.T)
        reflect = units[1] - apply_left(lower_inv, panel_1)
        mixed = apply_left(inverse, unit_cur - apply_left(lower_inv, basis_cur))
        current = current - jnp.dot(mixed.T, reflect, precision=HIGHEST_PRECISION)
        return current.reshape(matrix.shape)

    return local


def solution(mesh):
    return jax.shard_map(
        make_local(mesh.shape["rows"], mesh.shape["cols"]),
        mesh=mesh,
        in_specs=(P(None, "cols", "rows"),),
        out_specs=P(None, "cols", "rows"),
        check_vma=False,
    )
```

```python
import jax
import jax.numpy as jnp
from jax import lax
from jax.experimental import pallas as pl
from jax.sharding import PartitionSpec as P

HIGHEST_PRECISION = lax.Precision.HIGHEST


def inner_rows(left, right):
    return lax.dot_general(left, right, (((1,), (1,)), ((), ())), precision=HIGHEST_PRECISION)


def apply_left(square, right_side):
    return jnp.dot(square, right_side, precision=HIGHEST_PRECISION)


def butterfly_steps(size):
    if size < 2 or size & (size - 1):
        return None
    return [1 << k for k in range(size.bit_length() - 1)]


def butterfly_sum(x, axis, size, steps=None):
    every = butterfly_steps(size)
    if every is None:
        return x if steps == [] else lax.psum(x, axis)
    for step in every if steps is None else steps:
        x = x + lax.ppermute(x, axis, [(i, i ^ step) for i in range(size)])
    return x


def invert_near_identity(square):
    identity = jnp.eye(square.shape[0], dtype=jnp.float32)
    approx = square.T * (2.0 / (0.25 + 4.84))
    for _ in range(8):
        approx = apply_left(approx, 2.0 * identity - apply_left(square, approx))
    return approx


def _eliminate_kernel(head_ref, out_ref):
    size = out_ref.shape[0]
    wide = 2 * size
    rows = lax.broadcasted_iota(jnp.int32, (size, wide), 0)
    lanes = lax.broadcasted_iota(jnp.int32, (size, wide), 1)
    row_ids = lax.broadcasted_iota(jnp.int32, (size, 1), 0)
    work = head_ref[:, :wide]
    work = jnp.where(lanes < size, work, (lanes == rows + size).astype(jnp.float32))
    for j in range(size):
        row = work[j:j + 1, :]
        pivot = row[:, j:j + 1]
        scale = lax.rsqrt(pivot)
        scaled = row * scale
        weight = jnp.where(row_ids > j, work[:, j:j + 1] * scale, 0.0)
        work = jnp.where(rows == j, scaled, work - weight * scaled)
    out_ref[...] = work[:, size:]


def lower_inverse(head):
    size = head.shape[0]
    return pl.pallas_call(
        _eliminate_kernel, out_shape=jax.ShapeDtypeStruct((size, size), jnp.float32)
    )(head)


def spread_pair(block, axis, size):
    index = lax.axis_index(axis)
    have = block
    dist = size // 2
    while dist >= 2:
        got = lax.ppermute(
            have, axis, [(i, i + dist) for i in range(size) if i % (2 * dist) < 2]
        )
        have = jnp.where(index % (2 * dist) >= dist, got, have)
        dist //= 2
    other = lax.ppermute(have, axis, [(i, i ^ 1) for i in range(size)])
    even = index % 2 == 0
    return jnp.where(even, have, other), jnp.where(even, other, have)


def from_root(value, axis, size):
    index = lax.axis_index(axis)
    dist = size // 2
    while dist >= 1:
        got = lax.ppermute(
            value, axis, [(i, i + dist) for i in range(size) if i % (2 * dist) == 0]
        )
        value = jnp.where(index % (2 * dist) == dist, got, value)
        dist //= 2
    return value


def make_local(rows_size, cols_size):
    def local(matrix):
        block_count, width, local_rows = matrix.shape
        current = matrix.reshape(block_count * width, local_rows)
        global_rows = lax.axis_index("rows") * local_rows + jnp.arange(local_rows, dtype=jnp.int32)
        identity = jnp.eye(width, dtype=jnp.float32)
        lanes = jnp.arange(width, dtype=jnp.int32)[:, None]
        units = [
            (lanes == (global_rows - k * width)[None, :]).astype(jnp.float32) for k in range(2)
        ]

        if butterfly_steps(cols_size) is None:
            gathered = lax.all_gather(current, "cols")
            panel_0 = gathered[0]
            second = gathered[1]
            head = butterfly_sum(
                inner_rows(panel_0, jnp.concatenate([panel_0, units[0]])), "rows", rows_size
            )
        else:
            head = inner_rows(current, jnp.concatenate([current, units[0]]))
            head = butterfly_sum(from_root(head, "cols", cols_size), "rows", rows_size)
            panel_0, second = spread_pair(current, "cols", cols_size)

        both = jnp.concatenate([current, second])
        tail = jnp.concatenate([inner_rows(panel_0, both), inner_rows(units[0], both)], axis=1)
        steps = butterfly_steps(rows_size)
        tail = butterfly_sum(tail, "rows", rows_size, None if steps is None else steps[:-1])
        lower_inv, tail = lax.optimization_barrier((lower_inverse(head), tail))
        tail = butterfly_sum(tail, "rows", rows_size, None if steps is None else steps[-1:])
        top_rows = head[:, width:]
        basis_cur, basis_sec, unit_cur, unit_sec = (
            tail[:, i * width:(i + 1) * width] for i in range(4)
        )
        top_block = apply_left(lower_inv, top_rows)
        inverse = invert_near_identity(identity - top_block.T)
        reflect = units[0] - apply_left(lower_inv, panel_0)
        mixed = apply_left(inverse, unit_cur - apply_left(lower_inv, basis_cur))
        mixed_sec = apply_left(inverse, unit_sec - apply_left(lower_inv, basis_sec))
        current = current - jnp.dot(mixed.T, reflect, precision=HIGHEST_PRECISION)
        second = second - jnp.dot(mixed_sec.T, reflect, precision=HIGHEST_PRECISION)

        panel_1 = jnp.where((global_rows >= width)[None, :], second, jnp.zeros_like(second))
        head = butterfly_sum(
            inner_rows(panel_1, jnp.concatenate([panel_1, units[1]])), "rows", rows_size
        )
        tail = butterfly_sum(
            jnp.concatenate([inner_rows(panel_1, current), inner_rows(units[1], current)], axis=1),
            "rows",
            rows_size,
        )
        top_rows = head[:, width:]
        basis_cur, unit_cur = tail[:, :width], tail[:, width:]
        lower_inv = lower_inverse(head)
        top_block = apply_left(lower_inv, top_rows)
        inverse = invert_near_identity(identity - top_block.T)
        reflect = units[1] - apply_left(lower_inv, panel_1)
        mixed = apply_left(inverse, unit_cur - apply_left(lower_inv, basis_cur))
        current = current - jnp.dot(mixed.T, reflect, precision=HIGHEST_PRECISION)
        return current.reshape(matrix.shape)

    return local


def solution(mesh):
    return jax.shard_map(
        make_local(mesh.shape["rows"], mesh.shape["cols"]),
        mesh=mesh,
        in_specs=(P(None, "cols", "rows"),),
        out_specs=P(None, "cols", "rows"),
        check_vma=False,
    )
```

```python
import jax
import jax.numpy as jnp
from jax import lax
from jax.experimental import pallas as pl
from jax.sharding import PartitionSpec as P

HIGHEST_PRECISION = lax.Precision.HIGHEST


def inner_rows(left, right):
    return lax.dot_general(left, right, (((1,), (1,)), ((), ())), precision=HIGHEST_PRECISION)


def apply_left(square, right_side):
    return jnp.dot(square, right_side, precision=HIGHEST_PRECISION)


def butterfly_steps(size):
    if size < 2 or size & (size - 1):
        return None
    return [1 << k for k in range(size.bit_length() - 1)]


def butterfly_sum(x, axis, size, steps=None):
    every = butterfly_steps(size)
    if every is None:
        return x if steps == [] else lax.psum(x, axis)
    for step in every if steps is None else steps:
        x = x + lax.ppermute(x, axis, [(i, i ^ step) for i in range(size)])
    return x


def invert_near_identity(square):
    identity = jnp.eye(square.shape[0], dtype=jnp.float32)
    approx = square.T * (2.0 / (0.25 + 4.84))
    for _ in range(7):
        approx = apply_left(approx, 2.0 * identity - apply_left(square, approx))
    return approx


def _eliminate_kernel(head_ref, out_ref):
    size = out_ref.shape[0]
    wide = 2 * size
    rows = lax.broadcasted_iota(jnp.int32, (size, wide), 0)
    lanes = lax.broadcasted_iota(jnp.int32, (size, wide), 1)
    row_ids = lax.broadcasted_iota(jnp.int32, (size, 1), 0)
    work = head_ref[:, :wide]
    work = jnp.where(lanes < size, work, (lanes == rows + size).astype(jnp.float32))
    for j in range(size):
        row = work[j:j + 1, :]
        pivot = row[:, j:j + 1]
        scale = lax.rsqrt(pivot)
        scaled = row * scale
        weight = jnp.where(row_ids > j, work[:, j:j + 1] * scale, 0.0)
        work = jnp.where(rows == j, scaled, work - weight * scaled)
    out_ref[...] = work[:, size:]


def lower_inverse(head):
    size = head.shape[0]
    return pl.pallas_call(
        _eliminate_kernel, out_shape=jax.ShapeDtypeStruct((size, size), jnp.float32)
    )(head)


def spread_pair(block, axis, size):
    index = lax.axis_index(axis)
    have = block
    dist = size // 2
    while dist >= 2:
        got = lax.ppermute(
            have, axis, [(i, i + dist) for i in range(size) if i % (2 * dist) < 2]
        )
        have = jnp.where(index % (2 * dist) >= dist, got, have)
        dist //= 2
    other = lax.ppermute(have, axis, [(i, i ^ 1) for i in range(size)])
    even = index % 2 == 0
    return jnp.where(even, have, other), jnp.where(even, other, have)


def from_root(value, axis, size):
    index = lax.axis_index(axis)
    dist = size // 2
    while dist >= 1:
        got = lax.ppermute(
            value, axis, [(i, i + dist) for i in range(size) if i % (2 * dist) == 0]
        )
        value = jnp.where(index % (2 * dist) == dist, got, value)
        dist //= 2
    return value


def make_local(rows_size, cols_size):
    def local(matrix):
        block_count, width, local_rows = matrix.shape
        current = matrix.reshape(block_count * width, local_rows)
        global_rows = lax.axis_index("rows") * local_rows + jnp.arange(local_rows, dtype=jnp.int32)
        identity = jnp.eye(width, dtype=jnp.float32)
        lanes = jnp.arange(width, dtype=jnp.int32)[:, None]
        units = [
            (lanes == (global_rows - k * width)[None, :]).astype(jnp.float32) for k in range(2)
        ]

        if butterfly_steps(cols_size) is None:
            gathered = lax.all_gather(current, "cols")
            panel_0 = gathered[0]
            second = gathered[1]
            head = butterfly_sum(
                inner_rows(panel_0, jnp.concatenate([panel_0, units[0]])), "rows", rows_size
            )
        else:
            head = inner_rows(current, jnp.concatenate([current, units[0]]))
            head = butterfly_sum(from_root(head, "cols", cols_size), "rows", rows_size)
            panel_0, second = spread_pair(current, "cols", cols_size)

        both = jnp.concatenate([current, second])
        tail = jnp.concatenate([inner_rows(panel_0, both), inner_rows(units[0], both)], axis=1)
        steps = butterfly_steps(rows_size)
        tail = butterfly_sum(tail, "rows", rows_size, None if steps is None else steps[:-1])
        lower_inv, tail = lax.optimization_barrier((lower_inverse(head), tail))
        tail = butterfly_sum(tail, "rows", rows_size, None if steps is None else steps[-1:])
        top_rows = head[:, width:]
        basis_cur, basis_sec, unit_cur, unit_sec = (
            tail[:, i * width:(i + 1) * width] for i in range(4)
        )
        top_block = apply_left(lower_inv, top_rows)
        inverse = invert_near_identity(identity - top_block.T)
        reflect = units[0] - apply_left(lower_inv, panel_0)
        mixed = apply_left(inverse, unit_cur - apply_left(lower_inv, basis_cur))
        mixed_sec = apply_left(inverse, unit_sec - apply_left(lower_inv, basis_sec))
        current = current - jnp.dot(mixed.T, reflect, precision=HIGHEST_PRECISION)
        second = second - jnp.dot(mixed_sec.T, reflect, precision=HIGHEST_PRECISION)

        panel_1 = jnp.where((global_rows >= width)[None, :], second, jnp.zeros_like(second))
        head = butterfly_sum(
            inner_rows(panel_1, jnp.concatenate([panel_1, units[1]])), "rows", rows_size
        )
        tail = butterfly_sum(
            jnp.concatenate([inner_rows(panel_1, current), inner_rows(units[1], current)], axis=1),
            "rows",
            rows_size,
        )
        top_rows = head[:, width:]
        basis_cur, unit_cur = tail[:, :width], tail[:, width:]
        lower_inv = lower_inverse(head)
        top_block = apply_left(lower_inv, top_rows)
        inverse = invert_near_identity(identity - top_block.T)
        reflect = units[1] - apply_left(lower_inv, panel_1)
        mixed = apply_left(inverse, unit_cur - apply_left(lower_inv, basis_cur))
        current = current - jnp.dot(mixed.T, reflect, precision=HIGHEST_PRECISION)
        return current.reshape(matrix.shape)

    return local


def solution(mesh):
    return jax.shard_map(
        make_local(mesh.shape["rows"], mesh.shape["cols"]),
        mesh=mesh,
        in_specs=(P(None, "cols", "rows"),),
        out_specs=P(None, "cols", "rows"),
        check_vma=False,
    )
```

```python
import jax
import jax.numpy as jnp
from jax import lax
from jax.experimental import pallas as pl
from jax.sharding import PartitionSpec as P

HIGHEST_PRECISION = lax.Precision.HIGHEST


def inner_rows(left, right):
    return lax.dot_general(left, right, (((1,), (1,)), ((), ())), precision=HIGHEST_PRECISION)


def apply_left(square, right_side):
    return jnp.dot(square, right_side, precision=HIGHEST_PRECISION)


def butterfly_steps(size):
    if size < 2 or size & (size - 1):
        return None
    return [1 << k for k in range(size.bit_length() - 1)]


def butterfly_sum(x, axis, size, steps=None):
    every = butterfly_steps(size)
    if every is None:
        return x if steps == [] else lax.psum(x, axis)
    for step in every if steps is None else steps:
        x = x + lax.ppermute(x, axis, [(i, i ^ step) for i in range(size)])
    return x


def invert_near_identity(square):
    identity = jnp.eye(square.shape[0], dtype=jnp.float32)
    approx = square.T * (2.0 / (0.25 + 4.84))
    for _ in range(7):
        approx = apply_left(approx, 2.0 * identity - apply_left(square, approx))
    return approx


def _eliminate_kernel(head_ref, out_ref):
    size = out_ref.shape[0]
    wide = 2 * size
    rows = lax.broadcasted_iota(jnp.int32, (size, wide), 0)
    lanes = lax.broadcasted_iota(jnp.int32, (size, wide), 1)
    row_ids = lax.broadcasted_iota(jnp.int32, (size, 1), 0)
    work = head_ref[:, :wide]
    work = jnp.where(lanes < size, work, (lanes == rows + size).astype(jnp.float32))
    for j in range(size):
        row = work[j:j + 1, :]
        pivot = row[:, j:j + 1]
        scale = lax.rsqrt(pivot)
        scaled = row * scale
        weight = jnp.where(row_ids > j, work[:, j:j + 1] * scale, 0.0)
        work = jnp.where(rows == j, scaled, work - weight * scaled)
    out_ref[...] = work[:, size:]


def lower_inverse(head):
    size = head.shape[0]
    return pl.pallas_call(
        _eliminate_kernel, out_shape=jax.ShapeDtypeStruct((size, size), jnp.float32)
    )(head)


def spread_pair(block, axis, size):
    index = lax.axis_index(axis)
    have = block
    dist = size // 2
    while dist >= 2:
        got = lax.ppermute(
            have, axis, [(i, i + dist) for i in range(size) if i % (2 * dist) < 2]
        )
        have = jnp.where(index % (2 * dist) >= dist, got, have)
        dist //= 2
    other = lax.ppermute(have, axis, [(i, i ^ 1) for i in range(size)])
    even = index % 2 == 0
    return jnp.where(even, have, other), jnp.where(even, other, have)


def from_root(value, axis, size):
    index = lax.axis_index(axis)
    dist = size // 2
    while dist >= 1:
        got = lax.ppermute(
            value, axis, [(i, i + dist) for i in range(size) if i % (2 * dist) == 0]
        )
        value = jnp.where(index % (2 * dist) == dist, got, value)
        dist //= 2
    return value


def make_local(rows_size, cols_size):
    def local(matrix):
        block_count, width, local_rows = matrix.shape
        current = matrix.reshape(block_count * width, local_rows)
        global_rows = lax.axis_index("rows") * local_rows + jnp.arange(local_rows, dtype=jnp.int32)
        identity = jnp.eye(width, dtype=jnp.float32)
        lanes = jnp.arange(width, dtype=jnp.int32)[:, None]
        units = [
            (lanes == (global_rows - k * width)[None, :]).astype(jnp.float32) for k in range(2)
        ]

        if butterfly_steps(cols_size) is None:
            gathered = lax.all_gather(current, "cols")
            panel_0 = gathered[0]
            second = gathered[1]
            head = butterfly_sum(
                inner_rows(panel_0, jnp.concatenate([panel_0, units[0]])), "rows", rows_size
            )
        else:
            head = inner_rows(current, jnp.concatenate([current, units[0]]))
            head = butterfly_sum(from_root(head, "cols", cols_size), "rows", rows_size)
            panel_0, second = spread_pair(current, "cols", cols_size)

        both = jnp.concatenate([current, second])
        tail = jnp.concatenate([inner_rows(panel_0, both), inner_rows(units[0], both)], axis=1)
        steps = butterfly_steps(rows_size)
        tail = butterfly_sum(tail, "rows", rows_size, None if steps is None else steps[:-1])
        lower_inv, tail = lax.optimization_barrier((lower_inverse(head), tail))
        tail = butterfly_sum(tail, "rows", rows_size, None if steps is None else steps[-1:])
        top_rows = head[:, width:]
        basis_cur, basis_sec, unit_cur, unit_sec = (
            tail[:, i * width:(i + 1) * width] for i in range(4)
        )
        top_block = apply_left(lower_inv, top_rows)
        inverse = invert_near_identity(identity - top_block.T)
        reflect = units[0] - apply_left(lower_inv, panel_0)
        mixed = apply_left(inverse, unit_cur - apply_left(lower_inv, basis_cur))
        mixed_sec = apply_left(inverse, unit_sec - apply_left(lower_inv, basis_sec))
        current = current - jnp.dot(mixed.T, reflect, precision=HIGHEST_PRECISION)
        second = second - jnp.dot(mixed_sec.T, reflect, precision=HIGHEST_PRECISION)

        panel_1 = jnp.where((global_rows >= width)[None, :], second, jnp.zeros_like(second))
        head = butterfly_sum(
            inner_rows(panel_1, jnp.concatenate([panel_1, units[1]])), "rows", rows_size
        )
        tail = butterfly_sum(
            jnp.concatenate([inner_rows(panel_1, current), inner_rows(units[1], current)], axis=1),
            "rows",
            rows_size,
        )
        top_rows = head[:, width:]
        basis_cur, unit_cur = tail[:, :width], tail[:, width:]
        lower_inv = lower_inverse(head)
        top_block = apply_left(lower_inv, top_rows)
        inverse = invert_near_identity(identity - top_block.T)
        mixed = apply_left(inverse, unit_cur - apply_left(lower_inv, basis_cur))
        weights = jnp.concatenate([mixed, -jnp.dot(lower_inv.T, mixed, precision=HIGHEST_PRECISION)])
        current = current - lax.dot_general(
            weights, jnp.concatenate([units[1], panel_1]), (((0,), (0,)), ((), ())),
            precision=HIGHEST_PRECISION,
        )
        return current.reshape(matrix.shape)

    return local


def solution(mesh):
    return jax.shard_map(
        make_local(mesh.shape["rows"], mesh.shape["cols"]),
        mesh=mesh,
        in_specs=(P(None, "cols", "rows"),),
        out_specs=P(None, "cols", "rows"),
        check_vma=False,
    )
```

```python
import jax
import jax.numpy as jnp
from jax import lax
from jax.experimental import pallas as pl
from jax.sharding import PartitionSpec as P

HIGHEST_PRECISION = lax.Precision.HIGHEST


def inner_rows(left, right):
    return lax.dot_general(left, right, (((1,), (1,)), ((), ())), precision=HIGHEST_PRECISION)


def apply_left(square, right_side):
    return jnp.dot(square, right_side, precision=HIGHEST_PRECISION)


def butterfly_steps(size):
    if size < 2 or size & (size - 1):
        return None
    return [1 << k for k in range(size.bit_length() - 1)]


def butterfly_sum(x, axis, size, steps=None):
    every = butterfly_steps(size)
    if every is None:
        return x if steps == [] else lax.psum(x, axis)
    for step in every if steps is None else steps:
        x = x + lax.ppermute(x, axis, [(i, i ^ step) for i in range(size)])
    return x


def invert_near_identity(square):
    identity = jnp.eye(square.shape[0], dtype=jnp.float32)
    approx = square.T * (2.0 / (0.25 + 4.84))
    for _ in range(7):
        approx = apply_left(approx, 2.0 * identity - apply_left(square, approx))
    return approx


def _eliminate_kernel(head_ref, out_ref):
    size = out_ref.shape[0]
    wide = 2 * size
    rows = lax.broadcasted_iota(jnp.int32, (size, wide), 0)
    lanes = lax.broadcasted_iota(jnp.int32, (size, wide), 1)
    row_ids = lax.broadcasted_iota(jnp.int32, (size, 1), 0)
    work = head_ref[:, :wide]
    work = jnp.where(lanes < size, work, (lanes == rows + size).astype(jnp.float32))
    for j in range(size):
        row = work[j:j + 1, :]
        pivot = row[:, j:j + 1]
        scale = lax.rsqrt(pivot)
        scaled = row * scale
        weight = jnp.where(row_ids > j, work[:, j:j + 1] * scale, 0.0)
        work = jnp.where(rows == j, scaled, work - weight * scaled)
    out_ref[...] = work[:, size:]


def lower_inverse(head):
    size = head.shape[0]
    return pl.pallas_call(
        _eliminate_kernel, out_shape=jax.ShapeDtypeStruct((size, size), jnp.float32)
    )(head)


def spread_pair(block, axis, size):
    index = lax.axis_index(axis)
    have = block
    dist = size // 2
    while dist >= 2:
        got = lax.ppermute(
            have, axis, [(i, i + dist) for i in range(size) if i % (2 * dist) < 2]
        )
        have = jnp.where(index % (2 * dist) >= dist, got, have)
        dist //= 2
    other = lax.ppermute(have, axis, [(i, i ^ 1) for i in range(size)])
    even = index % 2 == 0
    return jnp.where(even, have, other), jnp.where(even, other, have)


def from_root(value, axis, size):
    index = lax.axis_index(axis)
    dist = size // 2
    while dist >= 1:
        got = lax.ppermute(
            value, axis, [(i, i + dist) for i in range(size) if i % (2 * dist) == 0]
        )
        value = jnp.where(index % (2 * dist) == dist, got, value)
        dist //= 2
    return value


def make_local(rows_size, cols_size):
    def local(matrix):
        block_count, width, local_rows = matrix.shape
        current = matrix.reshape(block_count * width, local_rows)
        global_rows = lax.axis_index("rows") * local_rows + jnp.arange(local_rows, dtype=jnp.int32)
        identity = jnp.eye(width, dtype=jnp.float32)
        lanes = jnp.arange(width, dtype=jnp.int32)[:, None]
        units = [
            (lanes == (global_rows - k * width)[None, :]).astype(jnp.float32) for k in range(2)
        ]

        if butterfly_steps(cols_size) is None:
            gathered = lax.all_gather(current, "cols")
            panel_0 = gathered[0]
            second = gathered[1]
            head = butterfly_sum(
                inner_rows(panel_0, jnp.concatenate([panel_0, units[0]])), "rows", rows_size
            )
        else:
            head = inner_rows(current, jnp.concatenate([current, units[0]]))
            head = butterfly_sum(from_root(head, "cols", cols_size), "rows", rows_size)
            panel_0, second = spread_pair(current, "cols", cols_size)

        both = jnp.concatenate([current, second])
        tail = jnp.concatenate([inner_rows(panel_0, both), inner_rows(units[0], both)], axis=1)
        steps = butterfly_steps(rows_size)
        tail = butterfly_sum(tail, "rows", rows_size, None if steps is None else steps[:-1])
        lower_inv, tail = lax.optimization_barrier((lower_inverse(head), tail))
        tail = butterfly_sum(tail, "rows", rows_size, None if steps is None else steps[-1:])
        top_rows = head[:, width:]
        basis_cur, basis_sec, unit_cur, unit_sec = (
            tail[:, i * width:(i + 1) * width] for i in range(4)
        )
        top_block = apply_left(lower_inv, top_rows)
        inverse = invert_near_identity(identity - top_block.T)
        reflect = units[0] - apply_left(lower_inv, panel_0)
        mixed = apply_left(inverse, unit_cur - apply_left(lower_inv, basis_cur))
        mixed_sec = apply_left(inverse, unit_sec - apply_left(lower_inv, basis_sec))
        current = current - jnp.dot(mixed.T, reflect, precision=HIGHEST_PRECISION)
        second = second - jnp.dot(mixed_sec.T, reflect, precision=HIGHEST_PRECISION)

        panel_1 = jnp.where((global_rows >= width)[None, :], second, jnp.zeros_like(second))
        head = butterfly_sum(
            inner_rows(panel_1, jnp.concatenate([panel_1, units[1]])), "rows", rows_size
        )
        tail = butterfly_sum(
            jnp.concatenate([inner_rows(panel_1, current), inner_rows(units[1], current)], axis=1),
            "rows",
            rows_size,
        )
        top_rows = head[:, width:]
        basis_cur, unit_cur = tail[:, :width], tail[:, width:]
        lower_inv = lower_inverse(head)
        top_block = apply_left(lower_inv, top_rows)
        inverse = invert_near_identity(identity - top_block.T)
        reflect = units[1] - jnp.dot(lower_inv, panel_1, precision=lax.Precision.HIGH)
        mixed = apply_left(inverse, unit_cur - apply_left(lower_inv, basis_cur))
        current = current - jnp.dot(mixed.T, reflect, precision=lax.Precision.HIGH)
        return current.reshape(matrix.shape)

    return local


def solution(mesh):
    return jax.shard_map(
        make_local(mesh.shape["rows"], mesh.shape["cols"]),
        mesh=mesh,
        in_specs=(P(None, "cols", "rows"),),
        out_specs=P(None, "cols", "rows"),
        check_vma=False,
    )
```

```python
import jax
import jax.numpy as jnp
from jax import lax
from jax.experimental import pallas as pl
from jax.sharding import PartitionSpec as P

HIGHEST_PRECISION = lax.Precision.HIGHEST


def inner_rows(left, right):
    return lax.dot_general(left, right, (((1,), (1,)), ((), ())), precision=HIGHEST_PRECISION)


def apply_left(square, right_side):
    return jnp.dot(square, right_side, precision=HIGHEST_PRECISION)


def butterfly_steps(size):
    if size < 2 or size & (size - 1):
        return None
    return [1 << k for k in range(size.bit_length() - 1)]


def butterfly_sum(x, axis, size, steps=None):
    every = butterfly_steps(size)
    if every is None:
        return x if steps == [] else lax.psum(x, axis)
    for step in every if steps is None else steps:
        x = x + lax.ppermute(x, axis, [(i, i ^ step) for i in range(size)])
    return x


def invert_near_identity(square):
    identity = jnp.eye(square.shape[0], dtype=jnp.float32)
    approx = square.T * (2.0 / (0.25 + 4.84))
    for _ in range(7):
        approx = apply_left(approx, 2.0 * identity - apply_left(square, approx))
    return approx


def _eliminate_kernel(head_ref, out_ref):
    size = out_ref.shape[0]
    wide = 2 * size
    rows = lax.broadcasted_iota(jnp.int32, (size, wide), 0)
    lanes = lax.broadcasted_iota(jnp.int32, (size, wide), 1)
    row_ids = lax.broadcasted_iota(jnp.int32, (size, 1), 0)
    work = head_ref[:, :wide]
    work = jnp.where(lanes < size, work, (lanes == rows + size).astype(jnp.float32))
    for j in range(size):
        row = work[j:j + 1, :]
        pivot = row[:, j:j + 1]
        scale = lax.rsqrt(pivot)
        scaled = row * scale
        weight = jnp.where(row_ids > j, work[:, j:j + 1] * scale, 0.0)
        work = jnp.where(rows == j, scaled, work - weight * scaled)
    out_ref[...] = work[:, size:]


def lower_inverse(head):
    size = head.shape[0]
    return pl.pallas_call(
        _eliminate_kernel, out_shape=jax.ShapeDtypeStruct((size, size), jnp.float32)
    )(head)


def spread_pair(block, axis, size):
    index = lax.axis_index(axis)
    have = block
    dist = size // 2
    while dist >= 2:
        got = lax.ppermute(
            have, axis, [(i, i + dist) for i in range(size) if i % (2 * dist) < 2]
        )
        have = jnp.where(index % (2 * dist) >= dist, got, have)
        dist //= 2
    other = lax.ppermute(have, axis, [(i, i ^ 1) for i in range(size)])
    even = index % 2 == 0
    return jnp.where(even, have, other), jnp.where(even, other, have)


def from_root(value, axis, size):
    index = lax.axis_index(axis)
    dist = size // 2
    while dist >= 1:
        got = lax.ppermute(
            value, axis, [(i, i + dist) for i in range(size) if i % (2 * dist) == 0]
        )
        value = jnp.where(index % (2 * dist) == dist, got, value)
        dist //= 2
    return value


def make_local(rows_size, cols_size):
    def local(matrix):
        block_count, width, local_rows = matrix.shape
        current = matrix.reshape(block_count * width, local_rows)
        global_rows = lax.axis_index("rows") * local_rows + jnp.arange(local_rows, dtype=jnp.int32)
        identity = jnp.eye(width, dtype=jnp.float32)
        lanes = jnp.arange(width, dtype=jnp.int32)[:, None]
        units = [
            (lanes == (global_rows - k * width)[None, :]).astype(jnp.float32) for k in range(2)
        ]

        if butterfly_steps(cols_size) is None:
            gathered = lax.all_gather(current, "cols")
            panel_0 = gathered[0]
            second = gathered[1]
            head = butterfly_sum(
                inner_rows(panel_0, jnp.concatenate([panel_0, units[0]])), "rows", rows_size
            )
        else:
            head = inner_rows(current, jnp.concatenate([current, units[0]]))
            head = butterfly_sum(from_root(head, "cols", cols_size), "rows", rows_size)
            panel_0, second = spread_pair(current, "cols", cols_size)

        both = jnp.concatenate([current, second])
        tail = jnp.concatenate([inner_rows(panel_0, both), inner_rows(units[0], both)], axis=1)
        steps = butterfly_steps(rows_size)
        tail = butterfly_sum(tail, "rows", rows_size, None if steps is None else steps[:-1])
        lower_inv = lower_inverse(head)
        inverse = invert_near_identity(identity - apply_left(lower_inv, head[:, width:]).T)
        lower_inv, inverse, tail = lax.optimization_barrier((lower_inv, inverse, tail))
        tail = butterfly_sum(tail, "rows", rows_size, None if steps is None else steps[-1:])
        basis_cur, basis_sec, unit_cur, unit_sec = (
            tail[:, i * width:(i + 1) * width] for i in range(4)
        )
        reflect = units[0] - apply_left(lower_inv, panel_0)
        mixed = apply_left(inverse, unit_cur - apply_left(lower_inv, basis_cur))
        mixed_sec = apply_left(inverse, unit_sec - apply_left(lower_inv, basis_sec))
        current = current - jnp.dot(mixed.T, reflect, precision=HIGHEST_PRECISION)
        second = second - jnp.dot(mixed_sec.T, reflect, precision=HIGHEST_PRECISION)

        panel_1 = jnp.where((global_rows >= width)[None, :], second, jnp.zeros_like(second))
        head = butterfly_sum(
            inner_rows(panel_1, jnp.concatenate([panel_1, units[1]])), "rows", rows_size
        )
        tail = butterfly_sum(
            jnp.concatenate([inner_rows(panel_1, current), inner_rows(units[1], current)], axis=1),
            "rows",
            rows_size,
        )
        top_rows = head[:, width:]
        basis_cur, unit_cur = tail[:, :width], tail[:, width:]
        lower_inv = lower_inverse(head)
        top_block = apply_left(lower_inv, top_rows)
        inverse = invert_near_identity(identity - top_block.T)
        reflect = units[1] - apply_left(lower_inv, panel_1)
        mixed = apply_left(inverse, unit_cur - apply_left(lower_inv, basis_cur))
        current = current - jnp.dot(mixed.T, reflect, precision=HIGHEST_PRECISION)
        return current.reshape(matrix.shape)

    return local


def solution(mesh):
    return jax.shard_map(
        make_local(mesh.shape["rows"], mesh.shape["cols"]),
        mesh=mesh,
        in_specs=(P(None, "cols", "rows"),),
        out_specs=P(None, "cols", "rows"),
        check_vma=False,
    )
```

```python
import jax
import jax.numpy as jnp
from jax import lax
from jax.experimental import pallas as pl
from jax.sharding import PartitionSpec as P

HIGHEST_PRECISION = lax.Precision.HIGHEST


def inner_rows(left, right):
    return lax.dot_general(left, right, (((1,), (1,)), ((), ())), precision=HIGHEST_PRECISION)


def apply_left(square, right_side):
    return jnp.dot(square, right_side, precision=HIGHEST_PRECISION)


def butterfly_steps(size):
    if size < 2 or size & (size - 1):
        return None
    return [1 << k for k in range(size.bit_length() - 1)]


def butterfly_sum(x, axis, size, steps=None):
    every = butterfly_steps(size)
    if every is None:
        return x if steps == [] else lax.psum(x, axis)
    for step in every if steps is None else steps:
        x = x + lax.ppermute(x, axis, [(i, i ^ step) for i in range(size)])
    return x


def invert_near_identity(square):
    identity = jnp.eye(square.shape[0], dtype=jnp.float32)
    approx = square.T * (2.0 / (0.25 + 4.84))
    for _ in range(7):
        approx = apply_left(approx, 2.0 * identity - apply_left(square, approx))
    return approx


def _eliminate_kernel(head_ref, out_ref):
    size = out_ref.shape[0]
    wide = 2 * size
    rows = lax.broadcasted_iota(jnp.int32, (size, wide), 0)
    lanes = lax.broadcasted_iota(jnp.int32, (size, wide), 1)
    row_ids = lax.broadcasted_iota(jnp.int32, (size, 1), 0)
    work = head_ref[:, :wide]
    work = jnp.where(lanes < size, work, (lanes == rows + size).astype(jnp.float32))
    for j in range(size):
        row = work[j:j + 1, :]
        pivot = row[:, j:j + 1]
        scale = lax.rsqrt(pivot)
        scaled = row * scale
        weight = jnp.where(row_ids > j, work[:, j:j + 1] * scale, 0.0)
        work = jnp.where(rows == j, scaled, work - weight * scaled)
    out_ref[...] = work[:, size:]


def lower_inverse(head):
    size = head.shape[0]
    return pl.pallas_call(
        _eliminate_kernel, out_shape=jax.ShapeDtypeStruct((size, size), jnp.float32)
    )(head)


def spread_pair(block, axis, size):
    index = lax.axis_index(axis)
    have = block
    dist = size // 2
    while dist >= 2:
        got = lax.ppermute(
            have, axis, [(i, i + dist) for i in range(size) if i % (2 * dist) < 2]
        )
        have = jnp.where(index % (2 * dist) >= dist, got, have)
        dist //= 2
    other = lax.ppermute(have, axis, [(i, i ^ 1) for i in range(size)])
    even = index % 2 == 0
    return jnp.where(even, have, other), jnp.where(even, other, have)


def from_root(value, axis, size):
    index = lax.axis_index(axis)
    dist = size // 2
    while dist >= 1:
        got = lax.ppermute(
            value, axis, [(i, i + dist) for i in range(size) if i % (2 * dist) == 0]
        )
        value = jnp.where(index % (2 * dist) == dist, got, value)
        dist //= 2
    return value


def make_local(rows_size, cols_size):
    def local(matrix):
        block_count, width, local_rows = matrix.shape
        current = matrix.reshape(block_count * width, local_rows)
        global_rows = lax.axis_index("rows") * local_rows + jnp.arange(local_rows, dtype=jnp.int32)
        identity = jnp.eye(width, dtype=jnp.float32)
        lanes = jnp.arange(width, dtype=jnp.int32)[:, None]
        units = [
            (lanes == (global_rows - k * width)[None, :]).astype(jnp.float32) for k in range(2)
        ]

        if butterfly_steps(cols_size) is None:
            gathered = lax.all_gather(current, "cols")
            panel_0 = gathered[0]
            second = gathered[1]
            head = butterfly_sum(
                inner_rows(panel_0, jnp.concatenate([panel_0, units[0]])), "rows", rows_size
            )
        else:
            head = inner_rows(current, jnp.concatenate([current, units[0]]))
            head = butterfly_sum(from_root(head, "cols", cols_size), "rows", rows_size)
            panel_0, second = spread_pair(current, "cols", cols_size)

        both = jnp.concatenate([current, second])
        tail = jnp.concatenate([inner_rows(panel_0, both), inner_rows(units[0], both)], axis=1)
        steps = butterfly_steps(rows_size)
        tail = butterfly_sum(tail, "rows", rows_size, None if steps is None else steps[:-1])
        lower_inv, tail = lax.optimization_barrier((lower_inverse(head), tail))
        tail = butterfly_sum(tail, "rows", rows_size, None if steps is None else steps[-1:])
        top_rows = head[:, width:]
        basis_cur, basis_sec, unit_cur, unit_sec = (
            tail[:, i * width:(i + 1) * width] for i in range(4)
        )
        top_block = apply_left(lower_inv, top_rows)
        inverse = invert_near_identity(identity - top_block.T)
        reflect = units[0] - apply_left(lower_inv, panel_0)
        mixed = apply_left(inverse, unit_cur - apply_left(lower_inv, basis_cur))
        mixed_sec = apply_left(inverse, unit_sec - apply_left(lower_inv, basis_sec))
        current = current - jnp.dot(mixed.T, reflect, precision=HIGHEST_PRECISION)
        second = second - jnp.dot(mixed_sec.T, reflect, precision=HIGHEST_PRECISION)

        panel_1 = jnp.where((global_rows >= width)[None, :], second, jnp.zeros_like(second))
        head = butterfly_sum(
            inner_rows(panel_1, jnp.concatenate([panel_1, units[1]])), "rows", rows_size
        )
        steps = butterfly_steps(rows_size)
        tail = butterfly_sum(
            jnp.concatenate([inner_rows(panel_1, current), inner_rows(units[1], current)], axis=1),
            "rows",
            rows_size,
            None if steps is None else steps[::-1],
        )
        top_rows = head[:, width:]
        basis_cur, unit_cur = tail[:, :width], tail[:, width:]
        lower_inv = lower_inverse(head)
        top_block = apply_left(lower_inv, top_rows)
        inverse = invert_near_identity(identity - top_block.T)
        reflect = units[1] - apply_left(lower_inv, panel_1)
        mixed = apply_left(inverse, unit_cur - apply_left(lower_inv, basis_cur))
        current = current - jnp.dot(mixed.T, reflect, precision=HIGHEST_PRECISION)
        return current.reshape(matrix.shape)

    return local


def solution(mesh):
    return jax.shard_map(
        make_local(mesh.shape["rows"], mesh.shape["cols"]),
        mesh=mesh,
        in_specs=(P(None, "cols", "rows"),),
        out_specs=P(None, "cols", "rows"),
        check_vma=False,
    )
```

```python
import jax
import jax.numpy as jnp
from jax import lax
from jax.experimental import pallas as pl
from jax.sharding import PartitionSpec as P

HIGHEST_PRECISION = lax.Precision.HIGHEST


def inner_rows(left, right):
    return lax.dot_general(left, right, (((1,), (1,)), ((), ())), precision=HIGHEST_PRECISION)


def apply_left(square, right_side):
    return jnp.dot(square, right_side, precision=HIGHEST_PRECISION)


def butterfly_steps(size):
    if size < 2 or size & (size - 1):
        return None
    return [1 << k for k in range(size.bit_length() - 1)]


def butterfly_sum(x, axis, size, steps=None):
    every = butterfly_steps(size)
    if every is None:
        return x if steps == [] else lax.psum(x, axis)
    for step in every if steps is None else steps:
        x = x + lax.ppermute(x, axis, [(i, i ^ step) for i in range(size)])
    return x


def invert_near_identity(square):
    identity = jnp.eye(square.shape[0], dtype=jnp.float32)
    approx = square.T * (2.0 / (0.25 + 4.84))
    for _ in range(7):
        approx = apply_left(approx, 2.0 * identity - apply_left(square, approx))
    return approx


def _eliminate_kernel(head_ref, out_ref):
    size = out_ref.shape[0]
    wide = 2 * size
    rows = lax.broadcasted_iota(jnp.int32, (size, wide), 0)
    lanes = lax.broadcasted_iota(jnp.int32, (size, wide), 1)
    row_ids = lax.broadcasted_iota(jnp.int32, (size, 1), 0)
    work = head_ref[:, :wide]
    work = jnp.where(lanes < size, work, (lanes == rows + size).astype(jnp.float32))
    for j in range(size):
        row = work[j:j + 1, :]
        pivot = row[:, j:j + 1]
        scale = lax.rsqrt(pivot)
        scaled = row * scale
        weight = jnp.where(row_ids > j, work[:, j:j + 1] * scale, 0.0)
        work = jnp.where(rows == j, scaled, work - weight * scaled)
    out_ref[...] = work[:, size:]


def lower_inverse(head):
    size = head.shape[0]
    return pl.pallas_call(
        _eliminate_kernel, out_shape=jax.ShapeDtypeStruct((size, size), jnp.float32)
    )(head)


def spread_pair(block, axis, size):
    index = lax.axis_index(axis)
    have = block
    dist = size // 2
    while dist >= 2:
        got = lax.ppermute(
            have, axis, [(i, i + dist) for i in range(size) if i % (2 * dist) < 2]
        )
        have = jnp.where(index % (2 * dist) >= dist, got, have)
        dist //= 2
    other = lax.ppermute(have, axis, [(i, i ^ 1) for i in range(size)])
    even = index % 2 == 0
    return jnp.where(even, have, other), jnp.where(even, other, have)


def from_root(value, axis, size):
    index = lax.axis_index(axis)
    dist = size // 2
    while dist >= 1:
        got = lax.ppermute(
            value, axis, [(i, i + dist) for i in range(size) if i % (2 * dist) == 0]
        )
        value = jnp.where(index % (2 * dist) == dist, got, value)
        dist //= 2
    return value


def make_local(rows_size, cols_size):
    def local(matrix):
        block_count, width, local_rows = matrix.shape
        current = matrix.reshape(block_count * width, local_rows)
        global_rows = lax.axis_index("rows") * local_rows + jnp.arange(local_rows, dtype=jnp.int32)
        identity = jnp.eye(width, dtype=jnp.float32)
        lanes = jnp.arange(width, dtype=jnp.int32)[:, None]
        units = [
            (lanes == (global_rows - k * width)[None, :]).astype(jnp.float32) for k in range(2)
        ]

        def top_of(block, k):
            if local_rows < 2 * width:
                return inner_rows(block, units[k])
            first = lax.axis_index("rows") == 0
            piece = block[:, k * width:(k + 1) * width]
            return jnp.where(first, piece, jnp.zeros_like(piece))

        if butterfly_steps(cols_size) is None:
            gathered = lax.all_gather(current, "cols")
            panel_0 = gathered[0]
            second = gathered[1]
            head = butterfly_sum(
                inner_rows(panel_0, jnp.concatenate([panel_0, units[0]])), "rows", rows_size
            )
        else:
            head = jnp.concatenate([inner_rows(current, current), top_of(current, 0)], axis=1)
            head = butterfly_sum(from_root(head, "cols", cols_size), "rows", rows_size)
            panel_0, second = spread_pair(current, "cols", cols_size)

        both = jnp.concatenate([current, second])
        tail = jnp.concatenate([inner_rows(panel_0, both), top_of(both, 0).T], axis=1)
        steps = butterfly_steps(rows_size)
        tail = butterfly_sum(tail, "rows", rows_size, None if steps is None else steps[:-1])
        lower_inv, tail = lax.optimization_barrier((lower_inverse(head), tail))
        tail = butterfly_sum(tail, "rows", rows_size, None if steps is None else steps[-1:])
        top_rows = head[:, width:]
        basis_cur, basis_sec, unit_cur, unit_sec = (
            tail[:, i * width:(i + 1) * width] for i in range(4)
        )
        top_block = apply_left(lower_inv, top_rows)
        inverse = invert_near_identity(identity - top_block.T)
        reflect = units[0] - apply_left(lower_inv, panel_0)
        mixed = apply_left(inverse, unit_cur - apply_left(lower_inv, basis_cur))
        mixed_sec = apply_left(inverse, unit_sec - apply_left(lower_inv, basis_sec))
        current = current - jnp.dot(mixed.T, reflect, precision=HIGHEST_PRECISION)
        second = second - jnp.dot(mixed_sec.T, reflect, precision=HIGHEST_PRECISION)

        panel_1 = jnp.where((global_rows >= width)[None, :], second, jnp.zeros_like(second))
        head = butterfly_sum(
            jnp.concatenate([inner_rows(panel_1, panel_1), top_of(panel_1, 1)], axis=1),
            "rows",
            rows_size,
        )
        tail = butterfly_sum(
            jnp.concatenate([inner_rows(panel_1, current), top_of(current, 1).T], axis=1),
            "rows",
            rows_size,
        )
        top_rows = head[:, width:]
        basis_cur, unit_cur = tail[:, :width], tail[:, width:]
        lower_inv = lower_inverse(head)
        top_block = apply_left(lower_inv, top_rows)
        inverse = invert_near_identity(identity - top_block.T)
        reflect = units[1] - apply_left(lower_inv, panel_1)
        mixed = apply_left(inverse, unit_cur - apply_left(lower_inv, basis_cur))
        current = current - jnp.dot(mixed.T, reflect, precision=HIGHEST_PRECISION)
        return current.reshape(matrix.shape)

    return local


def solution(mesh):
    return jax.shard_map(
        make_local(mesh.shape["rows"], mesh.shape["cols"]),
        mesh=mesh,
        in_specs=(P(None, "cols", "rows"),),
        out_specs=P(None, "cols", "rows"),
        check_vma=False,
    )
```
